128 devices in a mesh: grp: 8 (over x, core), mem: 16 (over z, y).
Axes of the slice: x: 4, y: 4, z: 4, core: 2. Of those that a mesh axis runs over, the one named last changes fastest.
Arguments:
- clips: bfloat16 [32768, 1152], P(('grp', 'mem')), may hold values from -6 to 6
- captions: bfloat16 [8192, 1152], P(('grp', 'mem')), may hold values from -6 to 6
- clip_bucket: int32 [32768], P(('grp', 'mem')), may hold values from 0 to 15, as said below
- clip_positive: int32 [32768], P(('grp', 'mem')), may hold values from 0 to 8191, as said below
- caption_bucket: int32 [8192], P(('grp', 'mem')), may hold values from 0 to 15, as said below
- bucket_owner: int32 [16], replicated, may hold values from 0 to 7, as said below
- scale: float32 [1], replicated, may hold values from 0.02 to 0.06
- bias: float32 [1], replicated, may hold values from -4 to -1
Outputs:
- clip_grad: float32 [32768, 1152], P(('grp', 'mem'))
- caption_grad: float32 [8192, 1152], P(('grp', 'mem'))
The draws below stay inside these ranges and needn't reach their ends.
Inputs may be any that keep to these rules, and one draw needn't show every extreme that they name: `bucket_owner`: each group owns exactly 2 buckets. `caption_bucket`: caption rows g * 1024 to (g + 1) * 1024 - 1 have buckets owned by group g, and every bucket has a caption. `clip_bucket`: within one device's block of 256 clip rows, among the rows whose offsets in the block are equal modulo the size of axis mem, at most 4 have buckets owned by one group; one group receives exactly 4 such rows from every such set of every device. `clip_positive`: each clip's own caption has the clip's bucket.
All inputs are finite; a program needn't handle non-finite values.
Results may differ from the reference program's by a relative error of at most 0.0027.
Values may be sent and summed in bfloat16 or wider, within the bound.
No kernel may reach another device: no remote copies, remote signals or barrier semaphores. Data moves between devices by JAX's collectives and lax.ppermute only.
A program may use at most 128 MiB of HBM per device.

```python
import math
import jax
import jax.numpy as jnp
from jax import lax

D = 1152
CLIP_DEV = 256
BPG = 2
CLIPS = 32768
CAPTIONS = 8192
PANEL = 1024
BUCKETS = 16
CAP = 4
SLOTS = 512
N_GRP = 8
N_MEM = 16


def layout(key):
    key_owner = jax.random.fold_in(key, 101)
    key_caption = jax.random.fold_in(key, 202)
    key_favored = jax.random.fold_in(key, 303)
    key_rank = jax.random.fold_in(key, 404)
    key_mix = jax.random.fold_in(key, 505)
    key_positive = jax.random.fold_in(key, 606)
    shuffled = jax.random.permutation(key_owner, BUCKETS).astype(jnp.int32)
    owner = (shuffled // BPG).astype(jnp.int32)
    slot_bucket = jnp.argsort(shuffled).astype(jnp.int32)
    cap_rows = jnp.arange(CAPTIONS, dtype=jnp.int32)
    within = cap_rows % PANEL
    picked = jax.random.randint(key_caption, (CAPTIONS,), 0, BPG, dtype=jnp.int32)
    local_slot = jnp.where(within < BPG, within, picked)
    caption_bucket = slot_bucket[cap_rows // PANEL * BPG + local_slot]
    devices = N_GRP * N_MEM
    per_lane = CLIP_DEV // N_MEM
    slot_count = N_GRP * CAP
    lanes = devices * N_MEM
    favored = jax.random.randint(key_favored, (), 0, N_GRP, dtype=jnp.int32)
    slot_ids = jnp.arange(slot_count, dtype=jnp.int32)
    noise = jax.random.randint(key_rank, (lanes, slot_count), 0, 1 << 20, dtype=jnp.int32)
    score = noise * slot_count + slot_ids[None, :]
    score = jnp.where((slot_ids // CAP == favored)[None, :], slot_ids[None, :] - slot_count, score)
    chosen = jnp.argsort(score, axis=1)[:, :per_lane].astype(jnp.int32)
    mixing = jax.random.randint(key_mix, (lanes, per_lane), 0, 1 << 20, dtype=jnp.int32)
    mixing = mixing * per_lane + jnp.arange(per_lane, dtype=jnp.int32)[None, :]
    chosen = jnp.take_along_axis(chosen, jnp.argsort(mixing, axis=1), axis=1)
    group = (chosen // CAP).astype(jnp.int32)
    group = group.reshape(devices, N_MEM, per_lane).transpose(0, 2, 1).reshape(CLIPS)
    offset = jax.random.randint(key_positive, (CLIPS,), 0, PANEL, dtype=jnp.int32)
    positive = (group * PANEL + offset).astype(jnp.int32)
    clip_bucket = caption_bucket[positive]
    return (owner, caption_bucket, clip_bucket, positive)


def draw_bucket_owner(key, part):
    return layout(key)[0]


def draw_caption_bucket(key, part):
    return layout(key)[1]


def draw_clip_bucket(key, part):
    return layout(key)[2]


def draw_clip_positive(key, part):
    return layout(key)[3]


def shard_levels(stream_key, shape, cuts, smallest, top_value):
    factor_of, own = 1.0, jax.random.fold_in(stream_key, 6)
    for axis_at, shards_of in cuts:
        draws = jnp.exp(jax.random.uniform(jax.random.fold_in(own, axis_at), (shards_of,), jnp.float32, smallest / len(cuts), top_value / len(cuts)))
        factor_of = factor_of * jnp.repeat(draws, shape[axis_at] // shards_of).reshape([-1 if axis == axis_at else 1 for axis in range(len(shape))])
    return factor_of


def normal_values(key, dims, scale, reach, cuts=(), held_as=jnp.bfloat16):
    level = shard_levels(key, dims, cuts, -0.22, 0.18) if cuts else 1.0
    drawn = jax.random.normal(key, dims, jnp.float32) * scale * level
    return jnp.minimum(jnp.maximum(drawn, -reach), reach).astype(held_as)


def setup_inputs(seed: int = 0) -> dict:
    key_list = jax.random.split(jax.random.key(seed), 9)
    clips = normal_values(key_list[0], (CLIPS, D), 1.0, 6.0, ((0, 128),))
    captions = normal_values(key_list[1], (CAPTIONS, D), 1.0, 6.0, ((0, 128),))
    clip_bucket = draw_clip_bucket(jax.random.fold_in(key_list[8], 71), 0)
    clip_positive = draw_clip_positive(jax.random.fold_in(key_list[8], 71), 0)
    caption_bucket = draw_caption_bucket(jax.random.fold_in(key_list[8], 71), 0)
    bucket_owner = draw_bucket_owner(jax.random.fold_in(key_list[8], 71), 0)
    scale = jnp.clip(jnp.exp(jax.random.uniform(key_list[6], (1,), jnp.float32, math.log(0.02), math.log(0.06))), 0.02, 0.06)
    bias = jnp.clip(jax.random.uniform(key_list[7], (1,), jnp.float32, -4.0, -1.0), -4.0, -1.0)
    return dict(clips=clips, captions=captions, clip_bucket=clip_bucket, clip_positive=clip_positive, caption_bucket=caption_bucket, bucket_owner=bucket_owner, scale=scale, bias=bias)


def reference(clips, captions, clip_bucket, clip_positive, caption_bucket, bucket_owner, scale, bias):
    window = min(CLIPS, SLOTS * N_MEM)
    owner_group = bucket_owner[clip_bucket].astype(jnp.int32)
    order = jnp.argsort(owner_group, stable=True).astype(jnp.int32)
    sorted_group = owner_group[order]
    starts = jnp.searchsorted(sorted_group, jnp.arange(N_GRP, dtype=jnp.int32)).astype(jnp.int32)
    mult = scale[0]
    shift = bias[0]

    def one_group(carry, group):
        clip_acc, cap_acc = carry
        first = jnp.minimum(starts[group], CLIPS - window).astype(jnp.int32)
        rows = lax.dynamic_slice_in_dim(order, first, window)
        inside = lax.dynamic_slice_in_dim(sorted_group, first, window) == group
        block_x = clips[rows]
        block_b = jnp.where(inside, clip_bucket[rows], -1)
        block_p = clip_positive[rows]
        cap_first = (group * PANEL).astype(jnp.int32)
        block_y = lax.dynamic_slice_in_dim(captions, cap_first, PANEL, 0)
        block_cb = lax.dynamic_slice_in_dim(caption_bucket, cap_first, PANEL)
        ids = cap_first + jnp.arange(PANEL, dtype=jnp.int32)
        logits = mult * jnp.dot(block_x, block_y.T, preferred_element_type=jnp.float32) + shift
        sign = jnp.where(block_p[:, None] == ids[None, :], 1.0, -1.0).astype(jnp.float32)
        same = block_b[:, None] == block_cb[None, :]
        weight = jnp.where(same, -sign * jax.nn.sigmoid(-sign * logits), 0.0).astype(jnp.bfloat16)
        grad_x = jnp.dot(weight, block_y, preferred_element_type=jnp.float32)
        grad_y = jnp.dot(weight.T, block_x, preferred_element_type=jnp.float32)
        grad_x = jnp.where(inside[:, None], grad_x, 0.0)
        clip_acc = clip_acc.at[rows].add(grad_x)
        old = lax.dynamic_slice_in_dim(cap_acc, cap_first, PANEL, 0)
        cap_acc = lax.dynamic_update_slice_in_dim(cap_acc, old + grad_y, cap_first, 0)
        return (clip_acc, cap_acc), None

    start_carry = (jnp.zeros((CLIPS, D), jnp.float32), jnp.zeros((CAPTIONS, D), jnp.float32))
    (clip_grad, caption_grad), _ = lax.scan(one_group, start_carry, jnp.arange(N_GRP, dtype=jnp.int32))
    return clip_grad, caption_grad
```

```python
import jax
import jax.numpy as jnp
from jax import lax
from jax.sharding import PartitionSpec as P


def pair_weights(logits, matched, same):
    sign = jnp.where(matched, 1.0, -1.0).astype(jnp.float32)
    return jnp.where(same, -sign * jax.nn.sigmoid(-sign * logits), 0.0).astype(jnp.bfloat16)


def inner_rows(left, right):
    return lax.dot_general(
        left, right, (((1,), (1,)), ((), ())), preferred_element_type=jnp.float32
    )


def body(clips, captions, clip_bucket, clip_positive, caption_bucket, bucket_owner, scale, bias):
    groups = lax.axis_size("grp")
    members = lax.axis_size("mem")
    clip_rows, width = clips.shape
    cap_rows = captions.shape[0]
    n_buckets = bucket_owner.shape[0]
    capacity = clip_rows // members * 4
    slots = capacity * groups
    panel = cap_rows * members
    code_base = panel * groups
    mult = scale[0]
    shift = bias[0]
    bucket_hot = clip_bucket[:, None] == jnp.arange(n_buckets, dtype=jnp.int32)[None, :]
    owner = jnp.sum(jnp.where(bucket_hot, bucket_owner[None, :], 0), axis=1)
    onehot = (owner[:, None] == jnp.arange(groups, dtype=jnp.int32)[None, :]).astype(jnp.int32)
    before = jnp.cumsum(onehot, axis=0) - onehot
    rank = jnp.sum(before * onehot, axis=1)
    position = owner * capacity + rank
    code = clip_bucket * code_base + clip_positive
    send_rows = jnp.zeros((slots, width), clips.dtype).at[position].set(clips)
    send_code = jnp.full((slots,), -1, jnp.int32).at[position].set(code)
    recv_rows = lax.all_to_all(send_rows, "grp", split_axis=0, concat_axis=0, tiled=True)
    recv_code = lax.all_to_all(send_code, "grp", split_axis=0, concat_axis=0, tiled=True)
    recv_bucket = jnp.where(recv_code >= 0, recv_code // code_base, -1)
    recv_positive = jnp.where(recv_code >= 0, recv_code % code_base, -1)
    group_index = lax.axis_index("grp")
    tag = jnp.broadcast_to(caption_bucket.astype(captions.dtype)[:, None], (cap_rows, 128))
    gathered = lax.all_gather(jnp.concatenate([captions, tag], axis=1), "mem", axis=0, tiled=True)
    rows_y = gathered[:, :width]
    bucket_y = gathered[:, width].astype(jnp.int32)
    count = rows_y.shape[0]
    logits = mult * inner_rows(recv_rows, rows_y) + shift
    ids = group_index * panel + jnp.arange(count, dtype=jnp.int32)
    weight = pair_weights(
        logits, recv_positive[:, None] == ids[None, :], recv_bucket[:, None] == bucket_y[None, :]
    )
    total = jnp.dot(weight, rows_y, preferred_element_type=jnp.float32).astype(jnp.bfloat16)
    caption_grad = lax.psum_scatter(
        lax.dot_general(
            weight, recv_rows, (((0,), (0,)), ((), ())), preferred_element_type=jnp.float32
        ),
        "mem",
        scatter_dimension=0,
        tiled=True,
    )
    returned = lax.all_to_all(total, "grp", split_axis=0, concat_axis=0, tiled=True)
    clip_grad = returned[position].astype(jnp.float32)
    return (clip_grad, caption_grad)


def solution(mesh):
    placed = (
        P(("grp", "mem"), None),
        P(("grp", "mem"), None),
        P(("grp", "mem")),
        P(("grp", "mem")),
        P(("grp", "mem")),
        P(),
        P(),
        P(),
    )
    return jax.shard_map(
        body,
        mesh=mesh,
        in_specs=placed,
        out_specs=(P(("grp", "mem"), None), P(("grp", "mem"), None)),
        check_vma=False,
    )
```

```python
import jax
import jax.numpy as jnp
from jax import lax
from jax.sharding import PartitionSpec as P


def pair_weights(logits, matched, same):
    sign = jnp.where(matched, 1.0, -1.0).astype(jnp.float32)
    return jnp.where(same, -sign * jax.nn.sigmoid(-sign * logits), 0.0).astype(jnp.bfloat16)


def inner_rows(left, right):
    return lax.dot_general(
        left, right, (((1,), (1,)), ((), ())), preferred_element_type=jnp.float32
    )


def body(clips, captions, clip_bucket, clip_positive, caption_bucket, bucket_owner, scale, bias):
    groups = lax.axis_size("grp")
    members = lax.axis_size("mem")
    clip_rows, width = clips.shape
    cap_rows = captions.shape[0]
    n_buckets = bucket_owner.shape[0]
    capacity = clip_rows // members * 4
    slots = capacity * groups
    panel = cap_rows * members
    code_base = panel * groups
    mult = scale[0]
    shift = bias[0]
    bucket_hot = clip_bucket[:, None] == jnp.arange(n_buckets, dtype=jnp.int32)[None, :]
    owner = jnp.sum(jnp.where(bucket_hot, bucket_owner[None, :], 0), axis=1)
    onehot = (owner[:, None] == jnp.arange(groups, dtype=jnp.int32)[None, :]).astype(jnp.int32)
    before = jnp.cumsum(onehot, axis=0) - onehot
    rank = jnp.sum(before * onehot, axis=1)
    position = owner * capacity + rank
    code = clip_bucket * code_base + clip_positive
    send_rows = jnp.zeros((slots, width), clips.dtype).at[position].set(clips)
    send_code = jnp.full((slots,), -1, jnp.int32).at[position].set(code)
    recv_rows = lax.all_to_all(send_rows, "grp", split_axis=0, concat_axis=0, tiled=True)
    recv_code = lax.all_to_all(send_code, "grp", split_axis=0, concat_axis=0, tiled=True)
    recv_bucket = jnp.where(recv_code >= 0, recv_code // code_base, -1)
    recv_positive = jnp.where(recv_code >= 0, recv_code % code_base, -1)
    group_index = lax.axis_index("grp")
    tag = jnp.broadcast_to(caption_bucket.astype(captions.dtype)[:, None], (cap_rows, 128))
    own = jnp.concatenate([captions, tag], axis=1)
    copies = jnp.broadcast_to(own[None], (members,) + own.shape).reshape(members * cap_rows, -1)
    gathered = lax.all_to_all(copies, "mem", split_axis=0, concat_axis=0, tiled=True)
    rows_y = gathered[:, :width]
    bucket_y = gathered[:, width].astype(jnp.int32)
    count = rows_y.shape[0]
    logits = mult * inner_rows(recv_rows, rows_y) + shift
    ids = group_index * panel + jnp.arange(count, dtype=jnp.int32)
    weight = pair_weights(
        logits, recv_positive[:, None] == ids[None, :], recv_bucket[:, None] == bucket_y[None, :]
    )
    total = jnp.dot(weight, rows_y, preferred_element_type=jnp.float32)
    partial = lax.dot_general(
        weight, recv_rows, (((0,), (0,)), ((), ())), preferred_element_type=jnp.float32
    )
    pieces = lax.all_to_all(partial, "mem", split_axis=0, concat_axis=0, tiled=True)
    caption_grad = jnp.sum(pieces.reshape(members, cap_rows, width), axis=0)
    returned = lax.all_to_all(total, "grp", split_axis=0, concat_axis=0, tiled=True)
    clip_grad = returned[position]
    return (clip_grad, caption_grad)


def solution(mesh):
    placed = (
        P(("grp", "mem"), None),
        P(("grp", "mem"), None),
        P(("grp", "mem")),
        P(("grp", "mem")),
        P(("grp", "mem")),
        P(),
        P(),
        P(),
    )
    return jax.shard_map(
        body,
        mesh=mesh,
        in_specs=placed,
        out_specs=(P(("grp", "mem"), None), P(("grp", "mem"), None)),
        check_vma=False,
    )
```

```python
import jax
import jax.numpy as jnp
from jax import lax
from jax.sharding import PartitionSpec as P


def pair_weights(logits, matched, same):
    sign = jnp.where(matched, 1.0, -1.0).astype(jnp.float32)
    return jnp.where(same, -sign * jax.nn.sigmoid(-sign * logits), 0.0).astype(jnp.bfloat16)


def inner_rows(left, right):
    return lax.dot_general(
        left, right, (((1,), (1,)), ((), ())), preferred_element_type=jnp.float32
    )


def shift_pairs(nz, ny, d, along_y):
    pairs = []
    for z in range(nz):
        for y in range(ny):
            if along_y:
                pairs.append((z * ny + y, z * ny + (y + d) % ny))
            else:
                pairs.append((z * ny + y, ((z + d) % nz) * ny + y))
    return pairs


def ring_gather(x, nz, ny, along_y):
    n = ny if along_y else nz
    parts = [x] + [lax.ppermute(x, "mem", shift_pairs(nz, ny, d, along_y)) for d in range(1, n)]
    return jnp.stack(parts)


def gather_2d(x, nz, ny, y_first):
    if y_first:
        inner = ring_gather(x, nz, ny, True)
        return ring_gather(inner, nz, ny, False)
    inner = ring_gather(x, nz, ny, False)
    return jnp.swapaxes(ring_gather(inner, nz, ny, True), 0, 1)


def ring_reduce(blocks, nz, ny, along_y):
    n = ny if along_y else nz
    total = blocks[0]
    for d in range(1, n):
        total = total + lax.ppermute(blocks[d], "mem", shift_pairs(nz, ny, -d, along_y))
    return total


def reduce_2d(blocks, nz, ny, z_first):
    if z_first:
        inner = ring_reduce(blocks, nz, ny, False)
        return ring_reduce(inner, nz, ny, True)
    inner = ring_reduce(jnp.swapaxes(blocks, 0, 1), nz, ny, True)
    return ring_reduce(inner, nz, ny, False)


def body(clips, captions, clip_bucket, clip_positive, caption_bucket, bucket_owner, scale, bias):
    groups = lax.axis_size("grp")
    members = lax.axis_size("mem")
    ny = int(round(members ** 0.5))
    nz = members // ny
    clip_rows, width = clips.shape
    cap_rows = captions.shape[0]
    half = cap_rows // 2
    n_buckets = bucket_owner.shape[0]
    capacity = clip_rows // members * 4
    slots = capacity * groups
    panel = cap_rows * members
    code_base = panel * groups
    mult = scale[0]
    shift = bias[0]
    bucket_hot = clip_bucket[:, None] == jnp.arange(n_buckets, dtype=jnp.int32)[None, :]
    owner = jnp.sum(jnp.where(bucket_hot, bucket_owner[None, :], 0), axis=1)
    onehot = (owner[:, None] == jnp.arange(groups, dtype=jnp.int32)[None, :]).astype(jnp.int32)
    before = jnp.cumsum(onehot, axis=0) - onehot
    rank = jnp.sum(before * onehot, axis=1)
    position = owner * capacity + rank
    code = clip_bucket * code_base + clip_positive
    send_rows = jnp.zeros((slots, width), clips.dtype).at[position].set(clips)
    send_code = jnp.full((slots,), -1, jnp.int32).at[position].set(code)
    recv_rows = lax.all_to_all(send_rows, "grp", split_axis=0, concat_axis=0, tiled=True)
    recv_code = lax.all_to_all(send_code, "grp", split_axis=0, concat_axis=0, tiled=True)
    recv_bucket = jnp.where(recv_code >= 0, recv_code // code_base, -1)
    recv_positive = jnp.where(recv_code >= 0, recv_code % code_base, -1)
    group_index = lax.axis_index("grp")
    member = lax.axis_index("mem")
    my_z = member // ny
    my_y = member % ny
    tag = jnp.broadcast_to(caption_bucket.astype(captions.dtype)[:, None], (cap_rows, 128))
    own = jnp.concatenate([captions, tag], axis=1)
    first = gather_2d(own[:half], nz, ny, True)
    second = gather_2d(own[half:], nz, ny, False)
    gathered = jnp.concatenate([first, second], axis=2).reshape(members * cap_rows, -1)
    rows_y = gathered[:, :width]
    bucket_y = gathered[:, width].astype(jnp.int32)
    count = rows_y.shape[0]
    dz = jnp.arange(nz, dtype=jnp.int32)[:, None, None]
    dy = jnp.arange(ny, dtype=jnp.int32)[None, :, None]
    src = ((my_z - dz) % nz) * ny + (my_y - dy) % ny
    ids = (group_index * panel + src * cap_rows + jnp.arange(cap_rows, dtype=jnp.int32)[None, None, :]).reshape(count)
    logits = mult * inner_rows(recv_rows, rows_y) + shift
    weight = pair_weights(
        logits, recv_positive[:, None] == ids[None, :], recv_bucket[:, None] == bucket_y[None, :]
    )
    total = jnp.dot(weight, rows_y, preferred_element_type=jnp.float32)
    partial = lax.dot_general(
        weight, recv_rows, (((0,), (0,)), ((), ())), preferred_element_type=jnp.float32
    ).reshape(nz, ny, cap_rows, width)
    grad_a = reduce_2d(partial[:, :, :half], nz, ny, True)
    grad_b = reduce_2d(partial[:, :, half:], nz, ny, False)
    caption_grad = jnp.concatenate([grad_a, grad_b], axis=0)
    returned = lax.all_to_all(total, "grp", split_axis=0, concat_axis=0, tiled=True)
    clip_grad = returned[position]
    return (clip_grad, caption_grad)


def solution(mesh):
    placed = (
        P(("grp", "mem"), None),
        P(("grp", "mem"), None),
        P(("grp", "mem")),
        P(("grp", "mem")),
        P(("grp", "mem")),
        P(),
        P(),
        P(),
    )
    return jax.shard_map(
        body,
        mesh=mesh,
        in_specs=placed,
        out_specs=(P(("grp", "mem"), None), P(("grp", "mem"), None)),
        check_vma=False,
    )
```

```python
import jax
import jax.numpy as jnp
from jax import lax
from jax.sharding import PartitionSpec as P


def pair_weights(logits, matched, same):
    sign = jnp.where(matched, 1.0, -1.0).astype(jnp.float32)
    return jnp.where(same, -sign * jax.nn.sigmoid(-sign * logits), 0.0).astype(jnp.bfloat16)


def inner_rows(left, right):
    return lax.dot_general(
        left, right, (((1,), (1,)), ((), ())), preferred_element_type=jnp.float32
    )


def inner_cols(left, right):
    return lax.dot_general(
        left, right, (((0,), (0,)), ((), ())), preferred_element_type=jnp.float32
    )


def shift_pairs(nz, ny, d, along_y):
    pairs = []
    for z in range(nz):
        for y in range(ny):
            if along_y:
                pairs.append((z * ny + y, z * ny + (y + d) % ny))
            else:
                pairs.append((z * ny + y, ((z + d) % nz) * ny + y))
    return pairs


def gather_pair(xa, xb, nz, ny):
    parts_a = [xa]
    parts_b = [xb]
    for d in range(1, ny):
        parts_a.append(lax.ppermute(xa, "mem", shift_pairs(nz, ny, d, True)))
        parts_b.append(lax.ppermute(xb, "mem", shift_pairs(nz, ny, d, False)))
    inner_a = jnp.stack(parts_a)
    inner_b = jnp.stack(parts_b)
    parts_a = [inner_a]
    parts_b = [inner_b]
    for d in range(1, nz):
        parts_a.append(lax.ppermute(inner_a, "mem", shift_pairs(nz, ny, d, False)))
        parts_b.append(lax.ppermute(inner_b, "mem", shift_pairs(nz, ny, d, True)))
    return jnp.stack(parts_a), jnp.stack(parts_b)


def reduce_pair(blocks_a, blocks_b, nz, ny):
    total_a = blocks_a[0]
    total_b = blocks_b[0]
    for d in range(1, nz):
        total_a = total_a + lax.ppermute(blocks_a[d], "mem", shift_pairs(nz, ny, -d, False))
        total_b = total_b + lax.ppermute(blocks_b[d], "mem", shift_pairs(nz, ny, -d, True))
    out_a = total_a[0]
    out_b = total_b[0]
    for d in range(1, ny):
        out_a = out_a + lax.ppermute(total_a[d], "mem", shift_pairs(nz, ny, -d, True))
        out_b = out_b + lax.ppermute(total_b[d], "mem", shift_pairs(nz, ny, -d, False))
    return out_a, out_b


def body(clips, captions, clip_bucket, clip_positive, caption_bucket, bucket_owner, scale, bias):
    groups = lax.axis_size("grp")
    members = lax.axis_size("mem")
    ny = int(round(members ** 0.5))
    nz = members // ny
    clip_rows, width = clips.shape
    cap_rows = captions.shape[0]
    half = cap_rows // 2
    n_buckets = bucket_owner.shape[0]
    capacity = clip_rows // members * 4
    slots = capacity * groups
    panel = cap_rows * members
    code_base = panel * groups
    mult = scale[0]
    shift = bias[0]
    bucket_hot = clip_bucket[:, None] == jnp.arange(n_buckets, dtype=jnp.int32)[None, :]
    owner = jnp.sum(jnp.where(bucket_hot, bucket_owner[None, :], 0), axis=1)
    onehot = (owner[:, None] == jnp.arange(groups, dtype=jnp.int32)[None, :]).astype(jnp.int32)
    before = jnp.cumsum(onehot, axis=0) - onehot
    rank = jnp.sum(before * onehot, axis=1)
    position = owner * capacity + rank
    code = clip_bucket * code_base + clip_positive
    send_rows = jnp.zeros((slots, width), clips.dtype).at[position].set(clips)
    send_code = jnp.full((slots,), -1, jnp.int32).at[position].set(code)
    recv_rows = lax.all_to_all(send_rows, "grp", split_axis=0, concat_axis=0, tiled=True)
    recv_code = lax.all_to_all(send_code, "grp", split_axis=0, concat_axis=0, tiled=True)
    recv_bucket = jnp.where(recv_code >= 0, recv_code // code_base, -1)
    recv_positive = jnp.where(recv_code >= 0, recv_code % code_base, -1)
    group_index = lax.axis_index("grp")
    member = lax.axis_index("mem")
    my_z = member // ny
    my_y = member % ny
    tag = jnp.broadcast_to(caption_bucket.astype(captions.dtype)[:, None], (cap_rows, 128))
    own = jnp.concatenate([captions, tag], axis=1)
    got_a, got_b = gather_pair(own[:half], own[half:], nz, ny)
    got_a = got_a.reshape(members * half, -1)
    got_b = got_b.reshape(members * half, -1)
    ar = jnp.arange(half, dtype=jnp.int32)
    za = jnp.arange(nz, dtype=jnp.int32)
    ya = jnp.arange(ny, dtype=jnp.int32)
    src_a = ((my_z - za[:, None]) % nz) * ny + (my_y - ya[None, :]) % ny
    src_b = ((my_z - za[None, :]) % nz) * ny + (my_y - ya[:, None]) % ny
    base = group_index * panel
    ids_a = (base + src_a[:, :, None] * cap_rows + ar[None, None, :]).reshape(-1)
    ids_b = (base + src_b[:, :, None] * cap_rows + half + ar[None, None, :]).reshape(-1)
    weights = []
    rows = []
    for got, ids in ((got_a, ids_a), (got_b, ids_b)):
        rows_y = got[:, :width]
        bucket_y = got[:, width].astype(jnp.int32)
        logits = mult * inner_rows(recv_rows, rows_y) + shift
        weights.append(pair_weights(
            logits, recv_positive[:, None] == ids[None, :], recv_bucket[:, None] == bucket_y[None, :]
        ))
        rows.append(rows_y)
    partial_a = inner_cols(weights[0], recv_rows).reshape(nz, ny, half, width)
    partial_b = inner_cols(weights[1], recv_rows).reshape(ny, nz, half, width)
    grad_a, grad_b = reduce_pair(partial_a, partial_b, nz, ny)
    total = (jnp.dot(weights[0], rows[0], preferred_element_type=jnp.float32)
             + jnp.dot(weights[1], rows[1], preferred_element_type=jnp.float32))
    returned = lax.all_to_all(total, "grp", split_axis=0, concat_axis=0, tiled=True)
    clip_grad = returned[position]
    caption_grad = jnp.concatenate([grad_a, grad_b], axis=0)
    return (clip_grad, caption_grad)


def solution(mesh):
    placed = (
        P(("grp", "mem"), None),
        P(("grp", "mem"), None),
        P(("grp", "mem")),
        P(("grp", "mem")),
        P(("grp", "mem")),
        P(),
        P(),
        P(),
    )
    return jax.shard_map(
        body,
        mesh=mesh,
        in_specs=placed,
        out_specs=(P(("grp", "mem"), None), P(("grp", "mem"), None)),
        check_vma=False,
    )
```

```python
import jax
import jax.numpy as jnp
from jax import lax
from jax.sharding import PartitionSpec as P


def pair_weights(logits, matched, same):
    sign = jnp.where(matched, 1.0, -1.0).astype(jnp.float32)
    return jnp.where(same, -sign * jax.nn.sigmoid(-sign * logits), 0.0).astype(jnp.bfloat16)


def inner_rows(left, right):
    return lax.dot_general(
        left, right, (((1,), (1,)), ((), ())), preferred_element_type=jnp.float32
    )


def inner_cols(left, right):
    return lax.dot_general(
        left, right, (((0,), (0,)), ((), ())), preferred_element_type=jnp.float32
    )


def shift_pairs(nz, ny, d, along_y):
    pairs = []
    for z in range(nz):
        for y in range(ny):
            if along_y:
                pairs.append((z * ny + y, z * ny + (y + d) % ny))
            else:
                pairs.append((z * ny + y, ((z + d) % nz) * ny + y))
    return pairs


def gather_first(xa, xb, nz, ny):
    parts_a = [xa]
    parts_b = [xb]
    for d in range(1, ny):
        parts_a.append(lax.ppermute(xa, "mem", shift_pairs(nz, ny, d, True)))
        parts_b.append(lax.ppermute(xb, "mem", shift_pairs(nz, ny, d, False)))
    return jnp.stack(parts_a), jnp.stack(parts_b)


def gather_second(inner_a, inner_b, nz, ny):
    parts_a = [inner_a]
    parts_b = [inner_b]
    for d in range(1, nz):
        parts_a.append(lax.ppermute(inner_a, "mem", shift_pairs(nz, ny, d, False)))
        parts_b.append(lax.ppermute(inner_b, "mem", shift_pairs(nz, ny, d, True)))
    return jnp.stack(parts_a), jnp.stack(parts_b)


def reduce_pair(blocks_a, blocks_b, nz, ny):
    total_a = blocks_a[0]
    total_b = blocks_b[0]
    for d in range(1, nz):
        total_a = total_a + lax.ppermute(blocks_a[d], "mem", shift_pairs(nz, ny, -d, False))
        total_b = total_b + lax.ppermute(blocks_b[d], "mem", shift_pairs(nz, ny, -d, True))
    out_a = total_a[0]
    out_b = total_b[0]
    for d in range(1, ny):
        out_a = out_a + lax.ppermute(total_a[d], "mem", shift_pairs(nz, ny, -d, True))
        out_b = out_b + lax.ppermute(total_b[d], "mem", shift_pairs(nz, ny, -d, False))
    return out_a, out_b


def body(clips, captions, clip_bucket, clip_positive, caption_bucket, bucket_owner, scale, bias):
    groups = lax.axis_size("grp")
    members = lax.axis_size("mem")
    ny = int(round(members ** 0.5))
    nz = members // ny
    clip_rows, width = clips.shape
    cap_rows = captions.shape[0]
    half = cap_rows // 2
    n_buckets = bucket_owner.shape[0]
    capacity = clip_rows // members * 4
    slots = capacity * groups
    panel = cap_rows * members
    code_base = panel * groups
    mult = scale[0]
    shift = bias[0]
    group_index = lax.axis_index("grp")
    member = lax.axis_index("mem")
    my_z = member // ny
    my_y = member % ny
    tag = jnp.broadcast_to(caption_bucket.astype(captions.dtype)[:, None], (cap_rows, 128))
    own = jnp.concatenate([captions, tag], axis=1)
    inner_a, inner_b = gather_first(own[:half], own[half:], nz, ny)
    inner_a, inner_b, clips, clip_bucket, clip_positive = lax.optimization_barrier(
        (inner_a, inner_b, clips, clip_bucket, clip_positive)
    )
    got_a, got_b = gather_second(inner_a, inner_b, nz, ny)
    bucket_hot = clip_bucket[:, None] == jnp.arange(n_buckets, dtype=jnp.int32)[None, :]
    owner = jnp.sum(jnp.where(bucket_hot, bucket_owner[None, :], 0), axis=1)
    onehot = (owner[:, None] == jnp.arange(groups, dtype=jnp.int32)[None, :]).astype(jnp.int32)
    before = jnp.cumsum(onehot, axis=0) - onehot
    rank = jnp.sum(before * onehot, axis=1)
    position = owner * capacity + rank
    code = clip_bucket * code_base + clip_positive
    send_rows = jnp.zeros((slots, width), clips.dtype).at[position].set(clips)
    send_code = jnp.full((slots,), -1, jnp.int32).at[position].set(code)
    recv_rows = lax.all_to_all(send_rows, "grp", split_axis=0, concat_axis=0, tiled=True)
    recv_code = lax.all_to_all(send_code, "grp", split_axis=0, concat_axis=0, tiled=True)
    recv_bucket = jnp.where(recv_code >= 0, recv_code // code_base, -1)
    recv_positive = jnp.where(recv_code >= 0, recv_code % code_base, -1)
    got_a = got_a.reshape(members * half, -1)
    got_b = got_b.reshape(members * half, -1)
    ar = jnp.arange(half, dtype=jnp.int32)
    za = jnp.arange(nz, dtype=jnp.int32)
    ya = jnp.arange(ny, dtype=jnp.int32)
    src_a = ((my_z - za[:, None]) % nz) * ny + (my_y - ya[None, :]) % ny
    src_b = ((my_z - za[None, :]) % nz) * ny + (my_y - ya[:, None]) % ny
    base = group_index * panel
    ids_a = (base + src_a[:, :, None] * cap_rows + ar[None, None, :]).reshape(-1)
    ids_b = (base + src_b[:, :, None] * cap_rows + half + ar[None, None, :]).reshape(-1)
    weights = []
    rows = []
    for got, ids in ((got_a, ids_a), (got_b, ids_b)):
        rows_y = got[:, :width]
        bucket_y = got[:, width].astype(jnp.int32)
        logits = mult * inner_rows(recv_rows, rows_y) + shift
        weights.append(pair_weights(
            logits, recv_positive[:, None] == ids[None, :], recv_bucket[:, None] == bucket_y[None, :]
        ))
        rows.append(rows_y)
    partial = inner_cols(jnp.concatenate(weights, axis=1), recv_rows)
    partial_a = partial[: members * half].reshape(nz, ny, half, width)
    partial_b = partial[members * half:].reshape(ny, nz, half, width)
    grad_a, grad_b = reduce_pair(partial_a, partial_b, nz, ny)
    total = (jnp.dot(weights[0], rows[0], preferred_element_type=jnp.float32)
             + jnp.dot(weights[1], rows[1], preferred_element_type=jnp.float32))
    returned = lax.all_to_all(total, "grp", split_axis=0, concat_axis=0, tiled=True)
    clip_grad = returned[position]
    caption_grad = jnp.concatenate([grad_a, grad_b], axis=0)
    return (clip_grad, caption_grad)


def solution(mesh):
    placed = (
        P(("grp", "mem"), None),
        P(("grp", "mem"), None),
        P(("grp", "mem")),
        P(("grp", "mem")),
        P(("grp", "mem")),
        P(),
        P(),
        P(),
    )
    return jax.shard_map(
        body,
        mesh=mesh,
        in_specs=placed,
        out_specs=(P(("grp", "mem"), None), P(("grp", "mem"), None)),
        check_vma=False,
    )
```

```python
import jax
import jax.numpy as jnp
from jax import lax
from jax.sharding import PartitionSpec as P


def pair_weights(logits, matched, same):
    sign = jnp.where(matched, 1.0, -1.0).astype(jnp.float32)
    return jnp.where(same, -sign * jax.nn.sigmoid(-sign * logits), 0.0).astype(jnp.bfloat16)


def inner_rows(left, right):
    return lax.dot_general(
        left, right, (((1,), (1,)), ((), ())), preferred_element_type=jnp.float32
    )


def inner_cols(left, right):
    return lax.dot_general(
        left, right, (((0,), (0,)), ((), ())), preferred_element_type=jnp.float32
    )


def shift_pairs(nz, ny, d, along_y):
    pairs = []
    for z in range(nz):
        for y in range(ny):
            if along_y:
                pairs.append((z * ny + y, z * ny + (y + d) % ny))
            else:
                pairs.append((z * ny + y, ((z + d) % nz) * ny + y))
    return pairs


def gather_first(xa, xb, nz, ny):
    parts_a = [xa]
    parts_b = [xb]
    for d in range(1, ny):
        parts_a.append(lax.ppermute(xa, "mem", shift_pairs(nz, ny, d, True)))
        parts_b.append(lax.ppermute(xb, "mem", shift_pairs(nz, ny, d, False)))
    return jnp.stack(parts_a), jnp.stack(parts_b)


def gather_second(inner_a, inner_b, nz, ny):
    parts_a = [inner_a]
    parts_b = [inner_b]
    for d in range(1, nz):
        parts_a.append(lax.ppermute(inner_a, "mem", shift_pairs(nz, ny, d, False)))
        parts_b.append(lax.ppermute(inner_b, "mem", shift_pairs(nz, ny, d, True)))
    return jnp.stack(parts_a), jnp.stack(parts_b)


def reduce_pair(blocks_a, blocks_b, nz, ny):
    total_a = blocks_a[0]
    total_b = blocks_b[0]
    for d in range(1, nz):
        total_a = total_a + lax.ppermute(blocks_a[d], "mem", shift_pairs(nz, ny, -d, False))
        total_b = total_b + lax.ppermute(blocks_b[d], "mem", shift_pairs(nz, ny, -d, True))
    out_a = total_a[0]
    out_b = total_b[0]
    for d in range(1, ny):
        out_a = out_a + lax.ppermute(total_a[d], "mem", shift_pairs(nz, ny, -d, True))
        out_b = out_b + lax.ppermute(total_b[d], "mem", shift_pairs(nz, ny, -d, False))
    return out_a, out_b


def body(clips, captions, clip_bucket, clip_positive, caption_bucket, bucket_owner, scale, bias):
    groups = lax.axis_size("grp")
    members = lax.axis_size("mem")
    ny = int(round(members ** 0.5))
    nz = members // ny
    clip_rows, width = clips.shape
    cap_rows = captions.shape[0]
    half = cap_rows // 2
    n_buckets = bucket_owner.shape[0]
    capacity = clip_rows // members * 4
    slots = capacity * groups
    panel = cap_rows * members
    code_base = panel * groups
    mult = scale[0]
    shift = bias[0]
    group_index = lax.axis_index("grp")
    member = lax.axis_index("mem")
    my_z = member // ny
    my_y = member % ny
    tag = jnp.broadcast_to(caption_bucket.astype(captions.dtype)[:, None], (cap_rows, 128))
    own = jnp.concatenate([captions, tag], axis=1)
    inner_a, inner_b = gather_first(own[:half], own[half:], nz, ny)
    inner_a, inner_b, clips, clip_bucket, clip_positive = lax.optimization_barrier(
        (inner_a, inner_b, clips, clip_bucket, clip_positive)
    )
    got_a, got_b = gather_second(inner_a, inner_b, nz, ny)
    bucket_hot = clip_bucket[:, None] == jnp.arange(n_buckets, dtype=jnp.int32)[None, :]
    owner = jnp.sum(jnp.where(bucket_hot, bucket_owner[None, :], 0), axis=1)
    onehot = (owner[:, None] == jnp.arange(groups, dtype=jnp.int32)[None, :]).astype(jnp.int32)
    before = jnp.cumsum(onehot, axis=0) - onehot
    rank = jnp.sum(before * onehot, axis=1)
    position = owner * capacity + rank
    code = clip_bucket * code_base + clip_positive
    send_rows = jnp.zeros((slots, width), clips.dtype).at[position].set(clips)
    send_code = jnp.full((slots,), -1, jnp.int32).at[position].set(code)
    recv_rows = lax.all_to_all(send_rows, "grp", split_axis=0, concat_axis=0, tiled=True)
    recv_code = lax.all_to_all(send_code, "grp", split_axis=0, concat_axis=0, tiled=True)
    recv_bucket = jnp.where(recv_code >= 0, recv_code // code_base, -1)
    recv_positive = jnp.where(recv_code >= 0, recv_code % code_base, -1)
    got_a = got_a.reshape(members * half, -1)
    got_b = got_b.reshape(members * half, -1)
    ar = jnp.arange(half, dtype=jnp.int32)
    za = jnp.arange(nz, dtype=jnp.int32)
    ya = jnp.arange(ny, dtype=jnp.int32)
    src_a = ((my_z - za[:, None]) % nz) * ny + (my_y - ya[None, :]) % ny
    src_b = ((my_z - za[None, :]) % nz) * ny + (my_y - ya[:, None]) % ny
    base = group_index * panel
    ids_a = (base + src_a[:, :, None] * cap_rows + ar[None, None, :]).reshape(-1)
    ids_b = (base + src_b[:, :, None] * cap_rows + half + ar[None, None, :]).reshape(-1)
    weights = []
    rows = []
    for got, ids in ((got_a, ids_a), (got_b, ids_b)):
        rows_y = got[:, :width]
        bucket_y = got[:, width].astype(jnp.int32)
        logits = mult * inner_rows(recv_rows, rows_y) + shift
        weights.append(pair_weights(
            logits, recv_positive[:, None] == ids[None, :], recv_bucket[:, None] == bucket_y[None, :]
        ))
        rows.append(rows_y)
    total = (jnp.dot(weights[0], rows[0], preferred_element_type=jnp.float32)
             + jnp.dot(weights[1], rows[1], preferred_element_type=jnp.float32))
    returned = lax.all_to_all(total.astype(jnp.bfloat16), "grp", split_axis=0, concat_axis=0, tiled=True)
    clip_grad = returned[position].astype(jnp.float32)
    weights, recv_rows, total = lax.optimization_barrier((weights, recv_rows, total))
    partial_a = inner_cols(weights[0], recv_rows).reshape(nz, ny, half, width)
    partial_b = inner_cols(weights[1], recv_rows).reshape(ny, nz, half, width)
    grad_a, grad_b = reduce_pair(partial_a, partial_b, nz, ny)
    caption_grad = jnp.concatenate([grad_a, grad_b], axis=0)
    return (clip_grad, caption_grad)


def solution(mesh):
    placed = (
        P(("grp", "mem"), None),
        P(("grp", "mem"), None),
        P(("grp", "mem")),
        P(("grp", "mem")),
        P(("grp", "mem")),
        P(),
        P(),
        P(),
    )
    return jax.shard_map(
        body,
        mesh=mesh,
        in_specs=placed,
        out_specs=(P(("grp", "mem"), None), P(("grp", "mem"), None)),
        check_vma=False,
    )
```

```python
import jax
import jax.numpy as jnp
from jax import lax
from jax.sharding import PartitionSpec as P


def pair_weights(logits, matched, same):
    sign = jnp.where(matched, 1.0, -1.0).astype(jnp.float32)
    return jnp.where(same, -sign * jax.nn.sigmoid(-sign * logits), 0.0).astype(jnp.bfloat16)


def inner_rows(left, right):
    return lax.dot_general(
        left, right, (((1,), (1,)), ((), ())), preferred_element_type=jnp.float32
    )


def inner_cols(left, right):
    return lax.dot_general(
        left, right, (((0,), (0,)), ((), ())), preferred_element_type=jnp.float32
    )


def shift_pairs(nz, ny, d, along_y):
    pairs = []
    for z in range(nz):
        for y in range(ny):
            if along_y:
                pairs.append((z * ny + y, z * ny + (y + d) % ny))
            else:
                pairs.append((z * ny + y, ((z + d) % nz) * ny + y))
    return pairs


def gather_first(xa, xb, nz, ny):
    parts_a = [xa]
    parts_b = [xb]
    for d in range(1, ny):
        parts_a.append(lax.ppermute(xa, "mem", shift_pairs(nz, ny, d, True)))
        parts_b.append(lax.ppermute(xb, "mem", shift_pairs(nz, ny, d, False)))
    return jnp.stack(parts_a), jnp.stack(parts_b)


def gather_second(inner_a, inner_b, nz, ny):
    parts_a = [inner_a]
    parts_b = [inner_b]
    for d in range(1, nz):
        parts_a.append(lax.ppermute(inner_a, "mem", shift_pairs(nz, ny, d, False)))
        parts_b.append(lax.ppermute(inner_b, "mem", shift_pairs(nz, ny, d, True)))
    return jnp.stack(parts_a), jnp.stack(parts_b)


def reduce_pair(blocks_a, blocks_b, nz, ny):
    total_a = blocks_a[0]
    total_b = blocks_b[0]
    for d in range(1, nz):
        total_a = total_a + lax.ppermute(blocks_a[d], "mem", shift_pairs(nz, ny, -d, False))
        total_b = total_b + lax.ppermute(blocks_b[d], "mem", shift_pairs(nz, ny, -d, True))
    out_a = total_a[0]
    out_b = total_b[0]
    for d in range(1, ny):
        out_a = out_a + lax.ppermute(total_a[d], "mem", shift_pairs(nz, ny, -d, True))
        out_b = out_b + lax.ppermute(total_b[d], "mem", shift_pairs(nz, ny, -d, False))
    return out_a, out_b


def body(clips, captions, clip_bucket, clip_positive, caption_bucket, bucket_owner, scale, bias):
    groups = lax.axis_size("grp")
    members = lax.axis_size("mem")
    ny = int(round(members ** 0.5))
    nz = members // ny
    clip_rows, width = clips.shape
    cap_rows = captions.shape[0]
    half = cap_rows // 2
    n_buckets = bucket_owner.shape[0]
    capacity = clip_rows // members * 4
    slots = capacity * groups
    panel = cap_rows * members
    mult = scale[0]
    shift = bias[0]
    group_index = lax.axis_index("grp")
    member = lax.axis_index("mem")
    my_z = member // ny
    my_y = member % ny
    tag = jnp.broadcast_to(caption_bucket.astype(captions.dtype)[:, None], (cap_rows, 128))
    own = jnp.concatenate([captions, tag], axis=1)
    inner_a, inner_b = gather_first(own[:half], own[half:], nz, ny)
    inner_a, inner_b, clips, clip_bucket, clip_positive = lax.optimization_barrier(
        (inner_a, inner_b, clips, clip_bucket, clip_positive)
    )
    got_a, got_b = gather_second(inner_a, inner_b, nz, ny)
    bucket_hot = clip_bucket[:, None] == jnp.arange(n_buckets, dtype=jnp.int32)[None, :]
    owner = jnp.sum(jnp.where(bucket_hot, bucket_owner[None, :], 0), axis=1)
    onehot = (owner[:, None] == jnp.arange(groups, dtype=jnp.int32)[None, :]).astype(jnp.int32)
    before = jnp.cumsum(onehot, axis=0) - onehot
    rank = jnp.sum(before * onehot, axis=1)
    position = owner * capacity + rank
    meta = jnp.stack(
        [clip_bucket + 1, clip_positive // 128, clip_positive % 128], axis=1
    ).astype(clips.dtype)
    extra = jnp.concatenate([jnp.zeros((clip_rows, 1), clips.dtype), meta,
                             jnp.zeros((clip_rows, 124), clips.dtype)], axis=1)
    send_rows = jnp.zeros((slots, width + 128), clips.dtype).at[position].set(
        jnp.concatenate([clips, extra], axis=1))
    recv_ext = lax.all_to_all(send_rows, "grp", split_axis=0, concat_axis=0, tiled=True)
    recv_rows = recv_ext[:, :width]
    recv_meta = recv_ext[:, width + 1:width + 4].astype(jnp.int32)
    recv_bucket = recv_meta[:, 0] - 1
    recv_positive = jnp.where(recv_bucket >= 0, recv_meta[:, 1] * 128 + recv_meta[:, 2], -1)
    got_a = got_a.reshape(members * half, -1)
    got_b = got_b.reshape(members * half, -1)
    ar = jnp.arange(half, dtype=jnp.int32)
    za = jnp.arange(nz, dtype=jnp.int32)
    ya = jnp.arange(ny, dtype=jnp.int32)
    src_a = ((my_z - za[:, None]) % nz) * ny + (my_y - ya[None, :]) % ny
    src_b = ((my_z - za[None, :]) % nz) * ny + (my_y - ya[:, None]) % ny
    base = group_index * panel
    ids_a = (base + src_a[:, :, None] * cap_rows + ar[None, None, :]).reshape(-1)
    ids_b = (base + src_b[:, :, None] * cap_rows + half + ar[None, None, :]).reshape(-1)
    weights = []
    rows = []
    for got, ids in ((got_a, ids_a), (got_b, ids_b)):
        rows_y = got[:, :width]
        bucket_y = got[:, width].astype(jnp.int32)
        logits = mult * inner_rows(recv_rows, rows_y) + shift
        weights.append(pair_weights(
            logits, recv_positive[:, None] == ids[None, :], recv_bucket[:, None] == bucket_y[None, :]
        ))
        rows.append(rows_y)
    total = (jnp.dot(weights[0], rows[0], preferred_element_type=jnp.float32)
             + jnp.dot(weights[1], rows[1], preferred_element_type=jnp.float32))
    returned = lax.all_to_all(total.astype(jnp.bfloat16), "grp", split_axis=0, concat_axis=0, tiled=True)
    clip_grad = returned[position].astype(jnp.float32)
    weights, recv_rows, total = lax.optimization_barrier((weights, recv_rows, total))
    partial_a = inner_cols(weights[0], recv_rows).reshape(nz, ny, half, width)
    partial_b = inner_cols(weights[1], recv_rows).reshape(ny, nz, half, width)
    grad_a, grad_b = reduce_pair(partial_a, partial_b, nz, ny)
    caption_grad = jnp.concatenate([grad_a, grad_b], axis=0)
    return (clip_grad, caption_grad)


def solution(mesh):
    placed = (
        P(("grp", "mem"), None),
        P(("grp", "mem"), None),
        P(("grp", "mem")),
        P(("grp", "mem")),
        P(("grp", "mem")),
        P(),
        P(),
        P(),
    )
    return jax.shard_map(
        body,
        mesh=mesh,
        in_specs=placed,
        out_specs=(P(("grp", "mem"), None), P(("grp", "mem"), None)),
        check_vma=False,
    )
```

```python
import jax
import jax.numpy as jnp
from jax import lax
from jax.sharding import PartitionSpec as P


def pair_weights(logits, matched, same):
    sign = jnp.where(matched, 1.0, -1.0).astype(jnp.float32)
    return jnp.where(same, -sign * jax.nn.sigmoid(-sign * logits), 0.0).astype(jnp.bfloat16)


def inner_rows(left, right):
    return lax.dot_general(
        left, right, (((1,), (1,)), ((), ())), preferred_element_type=jnp.float32
    )


def inner_cols(left, right):
    return lax.dot_general(
        left, right, (((0,), (0,)), ((), ())), preferred_element_type=jnp.float32
    )


def shift_pairs(nz, ny, d, along_y):
    pairs = []
    for z in range(nz):
        for y in range(ny):
            if along_y:
                pairs.append((z * ny + y, z * ny + (y + d) % ny))
            else:
                pairs.append((z * ny + y, ((z + d) % nz) * ny + y))
    return pairs


def gather_first(xa, xb, nz, ny):
    parts_a = [xa]
    parts_b = [xb]
    for d in range(1, ny):
        parts_a.append(lax.ppermute(xa, "mem", shift_pairs(nz, ny, d, True)))
        parts_b.append(lax.ppermute(xb, "mem", shift_pairs(nz, ny, d, False)))
    return jnp.stack(parts_a), jnp.stack(parts_b)


def gather_second(inner_a, inner_b, nz, ny):
    parts_a = [inner_a]
    parts_b = [inner_b]
    for d in range(1, nz):
        parts_a.append(lax.ppermute(inner_a, "mem", shift_pairs(nz, ny, d, False)))
        parts_b.append(lax.ppermute(inner_b, "mem", shift_pairs(nz, ny, d, True)))
    return jnp.stack(parts_a), jnp.stack(parts_b)


def reduce_pair(blocks_a, blocks_b, nz, ny):
    low = jnp.bfloat16
    total_a = blocks_a[0]
    total_b = blocks_b[0]
    for d in range(1, nz):
        total_a = total_a + lax.ppermute(blocks_a[d].astype(low), "mem", shift_pairs(nz, ny, -d, False)).astype(jnp.float32)
        total_b = total_b + lax.ppermute(blocks_b[d].astype(low), "mem", shift_pairs(nz, ny, -d, True)).astype(jnp.float32)
    out_a = total_a[0]
    out_b = total_b[0]
    for d in range(1, ny):
        out_a = out_a + lax.ppermute(total_a[d].astype(low), "mem", shift_pairs(nz, ny, -d, True)).astype(jnp.float32)
        out_b = out_b + lax.ppermute(total_b[d].astype(low), "mem", shift_pairs(nz, ny, -d, False)).astype(jnp.float32)
    return out_a, out_b


def body(clips, captions, clip_bucket, clip_positive, caption_bucket, bucket_owner, scale, bias):
    groups = lax.axis_size("grp")
    members = lax.axis_size("mem")
    ny = int(round(members ** 0.5))
    nz = members // ny
    clip_rows, width = clips.shape
    cap_rows = captions.shape[0]
    half = cap_rows // 2
    n_buckets = bucket_owner.shape[0]
    capacity = clip_rows // members * 4
    slots = capacity * groups
    panel = cap_rows * members
    mult = scale[0]
    shift = bias[0]
    group_index = lax.axis_index("grp")
    member = lax.axis_index("mem")
    my_z = member // ny
    my_y = member % ny
    tag = jnp.broadcast_to(caption_bucket.astype(captions.dtype)[:, None], (cap_rows, 128))
    own = jnp.concatenate([captions, tag], axis=1)
    inner_a, inner_b = gather_first(own[:half], own[half:], nz, ny)
    inner_a, inner_b, clips, clip_bucket, clip_positive = lax.optimization_barrier(
        (inner_a, inner_b, clips, clip_bucket, clip_positive)
    )
    got_a, got_b = gather_second(inner_a, inner_b, nz, ny)
    bucket_hot = clip_bucket[:, None] == jnp.arange(n_buckets, dtype=jnp.int32)[None, :]
    owner = jnp.sum(jnp.where(bucket_hot, bucket_owner[None, :], 0), axis=1)
    onehot = (owner[:, None] == jnp.arange(groups, dtype=jnp.int32)[None, :]).astype(jnp.int32)
    before = jnp.cumsum(onehot, axis=0) - onehot
    rank = jnp.sum(before * onehot, axis=1)
    position = owner * capacity + rank
    meta = jnp.stack(
        [clip_bucket + 1, clip_positive // 128, clip_positive % 128], axis=1
    ).astype(clips.dtype)
    extra = jnp.concatenate([jnp.zeros((clip_rows, 1), clips.dtype), meta,
                             jnp.zeros((clip_rows, 124), clips.dtype)], axis=1)
    send_rows = jnp.zeros((slots, width + 128), clips.dtype).at[position].set(
        jnp.concatenate([clips, extra], axis=1))
    recv_ext = lax.all_to_all(send_rows, "grp", split_axis=0, concat_axis=0, tiled=True)
    recv_rows = recv_ext[:, :width]
    recv_meta = recv_ext[:, width + 1:width + 4].astype(jnp.int32)
    recv_bucket = recv_meta[:, 0] - 1
    recv_positive = jnp.where(recv_bucket >= 0, recv_meta[:, 1] * 128 + recv_meta[:, 2], -1)
    got_a = got_a.reshape(members * half, -1)
    got_b = got_b.reshape(members * half, -1)
    ar = jnp.arange(half, dtype=jnp.int32)
    za = jnp.arange(nz, dtype=jnp.int32)
    ya = jnp.arange(ny, dtype=jnp.int32)
    src_a = ((my_z - za[:, None]) % nz) * ny + (my_y - ya[None, :]) % ny
    src_b = ((my_z - za[None, :]) % nz) * ny + (my_y - ya[:, None]) % ny
    base = group_index * panel
    ids_a = (base + src_a[:, :, None] * cap_rows + ar[None, None, :]).reshape(-1)
    ids_b = (base + src_b[:, :, None] * cap_rows + half + ar[None, None, :]).reshape(-1)
    weights = []
    rows = []
    for got, ids in ((got_a, ids_a), (got_b, ids_b)):
        rows_y = got[:, :width]
        bucket_y = got[:, width].astype(jnp.int32)
        logits = mult * inner_rows(recv_rows, rows_y) + shift
        weights.append(pair_weights(
            logits, recv_positive[:, None] == ids[None, :], recv_bucket[:, None] == bucket_y[None, :]
        ))
        rows.append(rows_y)
    total = (jnp.dot(weights[0], rows[0], preferred_element_type=jnp.float32)
             + jnp.dot(weights[1], rows[1], preferred_element_type=jnp.float32))
    returned = lax.all_to_all(total.astype(jnp.bfloat16), "grp", split_axis=0, concat_axis=0, tiled=True)
    clip_grad = returned[position].astype(jnp.float32)
    weights, recv_rows, total = lax.optimization_barrier((weights, recv_rows, total))
    partial_a = inner_cols(weights[0], recv_rows).reshape(nz, ny, half, width)
    partial_b = inner_cols(weights[1], recv_rows).reshape(ny, nz, half, width)
    grad_a, grad_b = reduce_pair(partial_a, partial_b, nz, ny)
    caption_grad = jnp.concatenate([grad_a, grad_b], axis=0)
    return (clip_grad, caption_grad)


def solution(mesh):
    placed = (
        P(("grp", "mem"), None),
        P(("grp", "mem"), None),
        P(("grp", "mem")),
        P(("grp", "mem")),
        P(("grp", "mem")),
        P(),
        P(),
        P(),
    )
    return jax.shard_map(
        body,
        mesh=mesh,
        in_specs=placed,
        out_specs=(P(("grp", "mem"), None), P(("grp", "mem"), None)),
        check_vma=False,
    )
```

```python
import jax
import jax.numpy as jnp
from jax import lax
from jax.sharding import PartitionSpec as P


def pair_weights(logits, matched, same):
    sign = jnp.where(matched, 1.0, -1.0).astype(jnp.float32)
    return jnp.where(same, -sign * jax.nn.sigmoid(-sign * logits), 0.0).astype(jnp.bfloat16)


def inner_rows(left, right):
    return lax.dot_general(
        left, right, (((1,), (1,)), ((), ())), preferred_element_type=jnp.float32
    )


def inner_cols(left, right):
    return lax.dot_general(
        left, right, (((0,), (0,)), ((), ())), preferred_element_type=jnp.float32
    )


def shift_pairs(nz, ny, d, along_y):
    pairs = []
    for z in range(nz):
        for y in range(ny):
            if along_y:
                pairs.append((z * ny + y, z * ny + (y + d) % ny))
            else:
                pairs.append((z * ny + y, ((z + d) % nz) * ny + y))
    return pairs


def gather_first(xa, xb, nz, ny):
    parts_a = [xa]
    parts_b = [xb]
    for d in range(1, ny):
        parts_a.append(lax.ppermute(xa, "mem", shift_pairs(nz, ny, d, True)))
        parts_b.append(lax.ppermute(xb, "mem", shift_pairs(nz, ny, d, False)))
    return jnp.stack(parts_a), jnp.stack(parts_b)


def gather_second(inner_a, inner_b, nz, ny):
    parts_a = [inner_a]
    parts_b = [inner_b]
    for d in range(1, nz):
        parts_a.append(lax.ppermute(inner_a, "mem", shift_pairs(nz, ny, d, False)))
        parts_b.append(lax.ppermute(inner_b, "mem", shift_pairs(nz, ny, d, True)))
    return jnp.stack(parts_a), jnp.stack(parts_b)


def reduce_pair(blocks_a, blocks_b, nz, ny):
    low = jnp.bfloat16
    total_a = blocks_a[0]
    total_b = blocks_b[0]
    for d in range(1, nz):
        total_a = total_a + lax.ppermute(blocks_a[d].astype(low), "mem", shift_pairs(nz, ny, -d, False)).astype(jnp.float32)
        total_b = total_b + lax.ppermute(blocks_b[d].astype(low), "mem", shift_pairs(nz, ny, -d, True)).astype(jnp.float32)
    out_a = total_a[0]
    out_b = total_b[0]
    for d in range(1, ny):
        out_a = out_a + lax.ppermute(total_a[d].astype(low), "mem", shift_pairs(nz, ny, -d, True)).astype(jnp.float32)
        out_b = out_b + lax.ppermute(total_b[d].astype(low), "mem", shift_pairs(nz, ny, -d, False)).astype(jnp.float32)
    return out_a, out_b


def inner_body(clips, captions, clip_bucket, clip_positive, caption_bucket, bucket_owner, scale, bias):
    groups = lax.axis_size("grp")
    members = lax.axis_size("mem")
    ny = int(round(members ** 0.5))
    nz = members // ny
    clip_rows, width = clips.shape
    cap_rows = captions.shape[0]
    half = cap_rows // 2
    n_buckets = bucket_owner.shape[0]
    capacity = clip_rows // members * 4
    slots = capacity * groups
    panel = cap_rows * members
    mult = scale[0]
    shift = bias[0]
    group_index = lax.axis_index("grp")
    member = lax.axis_index("mem")
    my_z = member // ny
    my_y = member % ny
    tag = jnp.broadcast_to(caption_bucket.astype(captions.dtype)[:, None], (cap_rows, 128))
    own = jnp.concatenate([captions, tag], axis=1)
    inner_a, inner_b = gather_first(own[:half], own[half:], nz, ny)
    got_a, got_b = gather_second(inner_a, inner_b, nz, ny)
    bucket_hot = clip_bucket[:, None] == jnp.arange(n_buckets, dtype=jnp.int32)[None, :]
    owner = jnp.sum(jnp.where(bucket_hot, bucket_owner[None, :], 0), axis=1)
    onehot = (owner[:, None] == jnp.arange(groups, dtype=jnp.int32)[None, :]).astype(jnp.int32)
    before = jnp.cumsum(onehot, axis=0) - onehot
    rank = jnp.sum(before * onehot, axis=1)
    position = owner * capacity + rank
    meta = jnp.stack(
        [clip_bucket + 1, clip_positive // 128, clip_positive % 128], axis=1
    ).astype(clips.dtype)
    extra = jnp.concatenate([jnp.zeros((clip_rows, 1), clips.dtype), meta,
                             jnp.zeros((clip_rows, 124), clips.dtype)], axis=1)
    send_rows = jnp.zeros((slots, width + 128), clips.dtype).at[position].set(
        jnp.concatenate([clips, extra], axis=1))
    recv_ext = lax.all_to_all(send_rows, "grp", split_axis=0, concat_axis=0, tiled=True)
    recv_rows = recv_ext[:, :width]
    recv_meta = recv_ext[:, width + 1:width + 4].astype(jnp.int32)
    recv_bucket = recv_meta[:, 0] - 1
    recv_positive = jnp.where(recv_bucket >= 0, recv_meta[:, 1] * 128 + recv_meta[:, 2], -1)
    got_a = got_a.reshape(members * half, -1)
    got_b = got_b.reshape(members * half, -1)
    ar = jnp.arange(half, dtype=jnp.int32)
    za = jnp.arange(nz, dtype=jnp.int32)
    ya = jnp.arange(ny, dtype=jnp.int32)
    src_a = ((my_z - za[:, None]) % nz) * ny + (my_y - ya[None, :]) % ny
    src_b = ((my_z - za[None, :]) % nz) * ny + (my_y - ya[:, None]) % ny
    base = group_index * panel
    ids_a = (base + src_a[:, :, None] * cap_rows + ar[None, None, :]).reshape(-1)
    ids_b = (base + src_b[:, :, None] * cap_rows + half + ar[None, None, :]).reshape(-1)
    weights = []
    rows = []
    for got, ids in ((got_a, ids_a), (got_b, ids_b)):
        rows_y = got[:, :width]
        bucket_y = got[:, width].astype(jnp.int32)
        logits = mult * inner_rows(recv_rows, rows_y) + shift
        weights.append(pair_weights(
            logits, recv_positive[:, None] == ids[None, :], recv_bucket[:, None] == bucket_y[None, :]
        ))
        rows.append(rows_y)
    total = (jnp.dot(weights[0], rows[0], preferred_element_type=jnp.float32)
             + jnp.dot(weights[1], rows[1], preferred_element_type=jnp.float32))
    returned = lax.all_to_all(total.astype(jnp.bfloat16), "grp", split_axis=0, concat_axis=0, tiled=True)
    clip_grad = returned[position].astype(jnp.float32)
    weights, recv_rows, total = lax.optimization_barrier((weights, recv_rows, total))
    partial_a = inner_cols(weights[0], recv_rows).reshape(nz, ny, half, width)
    partial_b = inner_cols(weights[1], recv_rows).reshape(ny, nz, half, width)
    grad_a, grad_b = reduce_pair(partial_a, partial_b, nz, ny)
    caption_grad = jnp.concatenate([grad_a, grad_b], axis=0)
    return (clip_grad, caption_grad)


def solution(mesh):
    placed = (
        P(("grp", "mem"), None),
        P(("grp", "mem"), None),
        P(("grp", "mem")),
        P(("grp", "mem")),
        P(("grp", "mem")),
        P(),
        P(),
        P(),
    )
    return jax.shard_map(
        inner_body,
        mesh=mesh,
        in_specs=placed,
        out_specs=(P(("grp", "mem"), None), P(("grp", "mem"), None)),
        check_vma=False,
    )
```

```python
import jax
import jax.numpy as jnp
from jax import lax
from jax.sharding import PartitionSpec as P


def pair_weights(logits, matched, same):
    sign = jnp.where(matched, 1.0, -1.0).astype(jnp.float32)
    return jnp.where(same, -sign * jax.nn.sigmoid(-sign * logits), 0.0).astype(jnp.bfloat16)


def inner_rows(left, right):
    return lax.dot_general(
        left, right, (((1,), (1,)), ((), ())), preferred_element_type=jnp.float32
    )


def inner_cols(left, right):
    return lax.dot_general(
        left, right, (((0,), (0,)), ((), ())), preferred_element_type=jnp.float32
    )


def shift_pairs(nz, ny, d, along_y):
    pairs = []
    for z in range(nz):
        for y in range(ny):
            if along_y:
                pairs.append((z * ny + y, z * ny + (y + d) % ny))
            else:
                pairs.append((z * ny + y, ((z + d) % nz) * ny + y))
    return pairs


def gather_first(xb, nz, ny):
    parts_b = [xb]
    for d in range(1, nz):
        parts_b.append(lax.ppermute(xb, "mem", shift_pairs(nz, ny, d, False)))
    return jnp.stack(parts_b)


def gather_second(inner_b, nz, ny):
    parts_b = [inner_b]
    for d in range(1, ny):
        parts_b.append(lax.ppermute(inner_b, "mem", shift_pairs(nz, ny, d, True)))
    return jnp.stack(parts_b)


def reduce_pair(blocks_a, blocks_b, nz, ny):
    low = jnp.bfloat16
    total_a = blocks_a[0]
    total_b = blocks_b[0]
    for d in range(1, nz):
        total_a = total_a + lax.ppermute(blocks_a[d].astype(low), "mem", shift_pairs(nz, ny, -d, False)).astype(jnp.float32)
        total_b = total_b + lax.ppermute(blocks_b[d].astype(low), "mem", shift_pairs(nz, ny, -d, True)).astype(jnp.float32)
    out_a = total_a[0]
    out_b = total_b[0]
    for d in range(1, ny):
        out_a = out_a + lax.ppermute(total_a[d].astype(low), "mem", shift_pairs(nz, ny, -d, True)).astype(jnp.float32)
        out_b = out_b + lax.ppermute(total_b[d].astype(low), "mem", shift_pairs(nz, ny, -d, False)).astype(jnp.float32)
    return out_a, out_b


def inner_body(clips, captions, clip_bucket, clip_positive, caption_bucket, bucket_owner, scale, bias):
    groups = lax.axis_size("grp")
    members = lax.axis_size("mem")
    ny = int(round(members ** 0.5))
    nz = members // ny
    clip_rows, width = clips.shape
    cap_rows = captions.shape[0]
    half = cap_rows // 2
    n_buckets = bucket_owner.shape[0]
    capacity = clip_rows // members * 4
    slots = capacity * groups
    panel = cap_rows * members
    mult = scale[0]
    shift = bias[0]
    group_index = lax.axis_index("grp")
    member = lax.axis_index("mem")
    my_z = member // ny
    my_y = member % ny
    tag = jnp.broadcast_to(caption_bucket.astype(captions.dtype)[:, None], (cap_rows, 128))
    own = jnp.concatenate([captions, tag], axis=1)
    got_a = lax.all_gather(own[:half], "mem", axis=0, tiled=True)
    got_b = gather_second(gather_first(own[half:], nz, ny), nz, ny)
    bucket_hot = clip_bucket[:, None] == jnp.arange(n_buckets, dtype=jnp.int32)[None, :]
    owner = jnp.sum(jnp.where(bucket_hot, bucket_owner[None, :], 0), axis=1)
    onehot = (owner[:, None] == jnp.arange(groups, dtype=jnp.int32)[None, :]).astype(jnp.int32)
    before = jnp.cumsum(onehot, axis=0) - onehot
    rank = jnp.sum(before * onehot, axis=1)
    position = owner * capacity + rank
    meta = jnp.stack(
        [clip_bucket + 1, clip_positive // 128, clip_positive % 128], axis=1
    ).astype(clips.dtype)
    extra = jnp.concatenate([jnp.zeros((clip_rows, 1), clips.dtype), meta,
                             jnp.zeros((clip_rows, 124), clips.dtype)], axis=1)
    placer = (position[:, None] == jnp.arange(slots, dtype=jnp.int32)[None, :]).astype(clips.dtype)
    send_rows = lax.dot_general(
        placer, jnp.concatenate([clips, extra], axis=1), (((0,), (0,)), ((), ())),
        preferred_element_type=jnp.float32,
    ).astype(clips.dtype)
    recv_ext = lax.all_to_all(send_rows, "grp", split_axis=0, concat_axis=0, tiled=True)
    recv_rows = recv_ext[:, :width]
    recv_meta = recv_ext[:, width + 1:width + 4].astype(jnp.int32)
    recv_bucket = recv_meta[:, 0] - 1
    recv_positive = jnp.where(recv_bucket >= 0, recv_meta[:, 1] * 128 + recv_meta[:, 2], -1)
    got_a = got_a.reshape(members * half, -1)
    got_b = got_b.reshape(members * half, -1)
    ar = jnp.arange(half, dtype=jnp.int32)
    za = jnp.arange(nz, dtype=jnp.int32)
    ya = jnp.arange(ny, dtype=jnp.int32)
    src_a = ((my_z - za[:, None]) % nz) * ny + (my_y - ya[None, :]) % ny
    src_b = ((my_z - za[None, :]) % nz) * ny + (my_y - ya[:, None]) % ny
    base = group_index * panel
    ids_a = (base + jnp.arange(members, dtype=jnp.int32)[:, None] * cap_rows + ar[None, :]).reshape(-1)
    ids_b = (base + src_b[:, :, None] * cap_rows + half + ar[None, None, :]).reshape(-1)
    weights = []
    rows = []
    for got, ids in ((got_a, ids_a), (got_b, ids_b)):
        rows_y = got[:, :width]
        bucket_y = got[:, width].astype(jnp.int32)
        logits = mult * inner_rows(recv_rows, rows_y) + shift
        weights.append(pair_weights(
            logits, recv_positive[:, None] == ids[None, :], recv_bucket[:, None] == bucket_y[None, :]
        ))
        rows.append(rows_y)
    total = (jnp.dot(weights[0], rows[0], preferred_element_type=jnp.float32)
             + jnp.dot(weights[1], rows[1], preferred_element_type=jnp.float32))
    returned = lax.all_to_all(total.astype(jnp.bfloat16), "grp", split_axis=0, concat_axis=0, tiled=True)
    clip_grad = jnp.dot(placer, returned, preferred_element_type=jnp.float32)
    weights, recv_rows, total = lax.optimization_barrier((weights, recv_rows, total))
    partial_a = jnp.take(
        inner_cols(weights[0], recv_rows).reshape(members, half, width), src_a.reshape(-1), axis=0
    ).reshape(nz, ny, half, width)
    partial_b = inner_cols(weights[1], recv_rows).reshape(ny, nz, half, width)
    grad_a, grad_b = reduce_pair(partial_a, partial_b, nz, ny)
    caption_grad = jnp.concatenate([grad_a, grad_b], axis=0)
    return (clip_grad, caption_grad)


def solution(mesh):
    placed = (
        P(("grp", "mem"), None),
        P(("grp", "mem"), None),
        P(("grp", "mem")),
        P(("grp", "mem")),
        P(("grp", "mem")),
        P(),
        P(),
        P(),
    )
    return jax.shard_map(
        inner_body,
        mesh=mesh,
        in_specs=placed,
        out_specs=(P(("grp", "mem"), None), P(("grp", "mem"), None)),
        check_vma=False,
    )
```

```python
import jax
import jax.numpy as jnp
from jax import lax
from jax.sharding import PartitionSpec as P


def pair_weights(logits, matched, same):
    sign = jnp.where(matched, 1.0, -1.0).astype(jnp.float32)
    return jnp.where(same, -sign * jax.nn.sigmoid(-sign * logits), 0.0).astype(jnp.bfloat16)


def inner_rows(left, right):
    return lax.dot_general(
        left, right, (((1,), (1,)), ((), ())), preferred_element_type=jnp.float32
    )


def inner_cols(left, right):
    return lax.dot_general(
        left, right, (((0,), (0,)), ((), ())), preferred_element_type=jnp.float32
    )


def shift_pairs(nz, ny, d, along_y):
    pairs = []
    for z in range(nz):
        for y in range(ny):
            if along_y:
                pairs.append((z * ny + y, z * ny + (y + d) % ny))
            else:
                pairs.append((z * ny + y, ((z + d) % nz) * ny + y))
    return pairs


def gather_first(xa, xb, nz, ny):
    parts_a = [xa]
    parts_b = [xb]
    for d in range(1, ny):
        parts_a.append(lax.ppermute(xa, "mem", shift_pairs(nz, ny, d, True)))
        parts_b.append(lax.ppermute(xb, "mem", shift_pairs(nz, ny, d, False)))
    return jnp.stack(parts_a), jnp.stack(parts_b)


def gather_second(inner_a, inner_b, nz, ny):
    parts_a = [inner_a]
    parts_b = [inner_b]
    for d in range(1, nz):
        parts_a.append(lax.ppermute(inner_a, "mem", shift_pairs(nz, ny, d, False)))
        parts_b.append(lax.ppermute(inner_b, "mem", shift_pairs(nz, ny, d, True)))
    return jnp.stack(parts_a), jnp.stack(parts_b)


def reduce_pair(blocks_a, blocks_b, nz, ny):
    low = jnp.bfloat16
    total_a = blocks_a[0]
    total_b = blocks_b[0]
    for d in range(1, nz):
        total_a = total_a + lax.ppermute(blocks_a[d].astype(low), "mem", shift_pairs(nz, ny, -d, False)).astype(jnp.float32)
        total_b = total_b + lax.ppermute(blocks_b[d].astype(low), "mem", shift_pairs(nz, ny, -d, True)).astype(jnp.float32)
    out_a = total_a[0]
    out_b = total_b[0]
    for d in range(1, ny):
        out_a = out_a + lax.ppermute(total_a[d].astype(low), "mem", shift_pairs(nz, ny, -d, True)).astype(jnp.float32)
        out_b = out_b + lax.ppermute(total_b[d].astype(low), "mem", shift_pairs(nz, ny, -d, False)).astype(jnp.float32)
    return out_a, out_b


def inner_body(clips, captions, clip_bucket, clip_positive, caption_bucket, bucket_owner, scale, bias):
    groups = lax.axis_size("grp")
    members = lax.axis_size("mem")
    ny = int(round(members ** 0.5))
    nz = members // ny
    clip_rows, width = clips.shape
    cap_rows = captions.shape[0]
    half = cap_rows // 2
    n_buckets = bucket_owner.shape[0]
    capacity = clip_rows // members * 4
    slots = capacity * groups
    panel = cap_rows * members
    mult = scale[0]
    shift = bias[0]
    group_index = lax.axis_index("grp")
    member = lax.axis_index("mem")
    my_z = member // ny
    my_y = member % ny
    tag = jnp.broadcast_to(caption_bucket.astype(captions.dtype)[:, None], (cap_rows, 128))
    own = jnp.concatenate([captions, tag], axis=1)
    inner_a, inner_b = gather_first(own[:half], own[half:], nz, ny)
    got_a, got_b = gather_second(inner_a, inner_b, nz, ny)
    bucket_hot = clip_bucket[:, None] == jnp.arange(n_buckets, dtype=jnp.int32)[None, :]
    owner = jnp.sum(jnp.where(bucket_hot, bucket_owner[None, :], 0), axis=1)
    onehot = (owner[:, None] == jnp.arange(groups, dtype=jnp.int32)[None, :]).astype(jnp.int32)
    before = jnp.cumsum(onehot, axis=0) - onehot
    rank = jnp.sum(before * onehot, axis=1)
    position = owner * capacity + rank
    meta = jnp.stack(
        [clip_bucket + 1, clip_positive // 128, clip_positive % 128], axis=1
    ).astype(clips.dtype)
    extra = jnp.concatenate([jnp.zeros((clip_rows, 1), clips.dtype), meta,
                             jnp.zeros((clip_rows, 124), clips.dtype)], axis=1)
    placer = (position[:, None] == jnp.arange(slots, dtype=jnp.int32)[None, :]).astype(clips.dtype)
    send_rows = lax.dot_general(
        placer, jnp.concatenate([clips, extra], axis=1), (((0,), (0,)), ((), ())),
        preferred_element_type=jnp.float32,
    ).astype(clips.dtype)
    recv_ext = lax.all_to_all(send_rows, "grp", split_axis=0, concat_axis=0, tiled=True)
    recv_rows = recv_ext[:, :width]
    recv_meta = recv_ext[:, width + 1:width + 4].astype(jnp.int32)
    recv_bucket = recv_meta[:, 0] - 1
    recv_positive = jnp.where(recv_bucket >= 0, recv_meta[:, 1] * 128 + recv_meta[:, 2], -1)
    got_a = got_a.reshape(members * half, -1)
    got_b = got_b.reshape(members * half, -1)
    ar = jnp.arange(half, dtype=jnp.int32)
    za = jnp.arange(nz, dtype=jnp.int32)
    ya = jnp.arange(ny, dtype=jnp.int32)
    src_a = ((my_z - za[:, None]) % nz) * ny + (my_y - ya[None, :]) % ny
    src_b = ((my_z - za[None, :]) % nz) * ny + (my_y - ya[:, None]) % ny
    base = group_index * panel
    ids_a = (base + src_a[:, :, None] * cap_rows + ar[None, None, :]).reshape(-1)
    ids_b = (base + src_b[:, :, None] * cap_rows + half + ar[None, None, :]).reshape(-1)
    weights = []
    rows = []
    for got, ids in ((got_a, ids_a), (got_b, ids_b)):
        rows_y = got[:, :width]
        bucket_y = got[:, width].astype(jnp.int32)
        logits = mult * inner_rows(recv_rows, rows_y) + shift
        weights.append(pair_weights(
            logits, recv_positive[:, None] == ids[None, :], recv_bucket[:, None] == bucket_y[None, :]
        ))
        rows.append(rows_y)
    partial_a = inner_cols(weights[0], recv_rows).reshape(nz, ny, half, width)
    partial_b = inner_cols(weights[1], recv_rows).reshape(ny, nz, half, width)
    weight_b, partial_b = lax.optimization_barrier((weights[1], partial_b))
    total = (jnp.dot(weights[0], rows[0], preferred_element_type=jnp.float32)
             + jnp.dot(weight_b, rows[1], preferred_element_type=jnp.float32))
    returned = lax.all_to_all(total.astype(jnp.bfloat16), "grp", split_axis=0, concat_axis=0, tiled=True)
    clip_grad = jnp.dot(placer, returned, preferred_element_type=jnp.float32)
    grad_a, grad_b = reduce_pair(partial_a, partial_b, nz, ny)
    caption_grad = jnp.concatenate([grad_a, grad_b], axis=0)
    return (clip_grad, caption_grad)


def solution(mesh):
    placed = (
        P(("grp", "mem"), None),
        P(("grp", "mem"), None),
        P(("grp", "mem")),
        P(("grp", "mem")),
        P(("grp", "mem")),
        P(),
        P(),
        P(),
    )
    return jax.shard_map(
        inner_body,
        mesh=mesh,
        in_specs=placed,
        out_specs=(P(("grp", "mem"), None), P(("grp", "mem"), None)),
        check_vma=False,
    )
```

```python
import jax
import jax.numpy as jnp
from jax import lax
from jax.sharding import PartitionSpec as P


def pair_weights(logits, matched, same):
    sign = jnp.where(matched, 1.0, -1.0).astype(jnp.float32)
    return jnp.where(same, -sign * jax.nn.sigmoid(-sign * logits), 0.0).astype(jnp.bfloat16)


def inner_rows(left, right):
    return lax.dot_general(
        left, right, (((1,), (1,)), ((), ())), preferred_element_type=jnp.float32
    )


def inner_cols(left, right):
    return lax.dot_general(
        left, right, (((0,), (0,)), ((), ())), preferred_element_type=jnp.float32
    )


def shift_pairs(nz, ny, d, along_y):
    pairs = []
    for z in range(nz):
        for y in range(ny):
            if along_y:
                pairs.append((z * ny + y, z * ny + (y + d) % ny))
            else:
                pairs.append((z * ny + y, ((z + d) % nz) * ny + y))
    return pairs


def gather_first(xa, xb, nz, ny):
    parts_a = [xa]
    parts_b = [xb]
    for d in range(1, ny):
        parts_a.append(lax.ppermute(xa, "mem", shift_pairs(nz, ny, d, True)))
        parts_b.append(lax.ppermute(xb, "mem", shift_pairs(nz, ny, d, False)))
    return jnp.stack(parts_a), jnp.stack(parts_b)


def gather_second(inner_a, inner_b, nz, ny):
    parts_a = [inner_a]
    parts_b = [inner_b]
    for d in range(1, nz):
        parts_a.append(lax.ppermute(inner_a, "mem", shift_pairs(nz, ny, d, False)))
        parts_b.append(lax.ppermute(inner_b, "mem", shift_pairs(nz, ny, d, True)))
    return jnp.stack(parts_a), jnp.stack(parts_b)


def reduce_pair(blocks_a, blocks_b, nz, ny):
    low = jnp.bfloat16
    total_a = blocks_a[0]
    total_b = blocks_b[0]
    for d in range(1, nz):
        total_a = total_a + lax.ppermute(blocks_a[d].astype(low), "mem", shift_pairs(nz, ny, -d, False)).astype(jnp.float32)
        total_b = total_b + lax.ppermute(blocks_b[d].astype(low), "mem", shift_pairs(nz, ny, -d, True)).astype(jnp.float32)
    out_a = total_a[0]
    out_b = total_b[0]
    for d in range(1, ny):
        out_a = out_a + lax.ppermute(total_a[d].astype(low), "mem", shift_pairs(nz, ny, -d, True)).astype(jnp.float32)
        out_b = out_b + lax.ppermute(total_b[d].astype(low), "mem", shift_pairs(nz, ny, -d, False)).astype(jnp.float32)
    return out_a, out_b


def inner_body(clips, captions, clip_bucket, clip_positive, caption_bucket, bucket_owner, scale, bias):
    groups = lax.axis_size("grp")
    members = lax.axis_size("mem")
    ny = int(round(members ** 0.5))
    nz = members // ny
    clip_rows, width = clips.shape
    cap_rows = captions.shape[0]
    half = cap_rows // 2
    n_buckets = bucket_owner.shape[0]
    capacity = clip_rows // members * 4
    slots = capacity * groups
    panel = cap_rows * members
    mult = scale[0]
    shift = bias[0]
    group_index = lax.axis_index("grp")
    member = lax.axis_index("mem")
    my_z = member // ny
    my_y = member % ny
    tag = jnp.broadcast_to(caption_bucket.astype(captions.dtype)[:, None], (cap_rows, 128))
    own = jnp.concatenate([captions, tag], axis=1)
    inner_a, inner_b = gather_first(own[:half], own[half:], nz, ny)
    got_a, got_b = gather_second(inner_a, inner_b, nz, ny)
    bucket_hot = clip_bucket[:, None] == jnp.arange(n_buckets, dtype=jnp.int32)[None, :]
    owner = jnp.sum(jnp.where(bucket_hot, bucket_owner[None, :], 0), axis=1)
    onehot = (owner[:, None] == jnp.arange(groups, dtype=jnp.int32)[None, :]).astype(jnp.int32)
    before = jnp.cumsum(onehot, axis=0) - onehot
    rank = jnp.sum(before * onehot, axis=1)
    position = owner * capacity + rank
    meta = jnp.stack(
        [clip_bucket + 1, clip_positive // 128, clip_positive % 128], axis=1
    ).astype(clips.dtype)
    extra = jnp.concatenate([jnp.zeros((clip_rows, 1), clips.dtype), meta,
                             jnp.zeros((clip_rows, 124), clips.dtype)], axis=1)
    placer = (position[:, None] == jnp.arange(slots, dtype=jnp.int32)[None, :]).astype(clips.dtype)
    send_rows = lax.dot_general(
        placer, jnp.concatenate([clips, extra], axis=1), (((0,), (0,)), ((), ())),
        preferred_element_type=jnp.float32,
    ).astype(clips.dtype)
    recv_ext = lax.all_to_all(send_rows, "grp", split_axis=0, concat_axis=0, tiled=True)
    recv_rows = recv_ext[:, :width]
    recv_meta = recv_ext[:, width + 1:width + 4].astype(jnp.int32)
    recv_bucket = recv_meta[:, 0] - 1
    recv_positive = jnp.where(recv_bucket >= 0, recv_meta[:, 1] * 128 + recv_meta[:, 2], -1)
    got_a = got_a.reshape(members * half, -1)
    got_b = got_b.reshape(members * half, -1)
    ar = jnp.arange(half, dtype=jnp.int32)
    za = jnp.arange(nz, dtype=jnp.int32)
    ya = jnp.arange(ny, dtype=jnp.int32)
    src_a = ((my_z - za[:, None]) % nz) * ny + (my_y - ya[None, :]) % ny
    src_b = ((my_z - za[None, :]) % nz) * ny + (my_y - ya[:, None]) % ny
    base = group_index * panel
    ids_a = (base + src_a[:, :, None] * cap_rows + ar[None, None, :]).reshape(-1)
    ids_b = (base + src_b[:, :, None] * cap_rows + half + ar[None, None, :]).reshape(-1)
    weights = []
    rows = []
    for got, ids in ((got_a, ids_a), (got_b, ids_b)):
        rows_y = got[:, :width]
        bucket_y = got[:, width].astype(jnp.int32)
        logits = mult * inner_rows(recv_rows, rows_y) + shift
        weights.append(pair_weights(
            logits, recv_positive[:, None] == ids[None, :], recv_bucket[:, None] == bucket_y[None, :]
        ))
        rows.append(rows_y)
    total = (jnp.dot(weights[0], rows[0], preferred_element_type=jnp.float32)
             + jnp.dot(weights[1], rows[1], preferred_element_type=jnp.float32))
    returned = lax.all_to_all(total.astype(jnp.bfloat16), "grp", split_axis=0, concat_axis=0, tiled=True)
    clip_grad = jnp.dot(placer, returned, preferred_element_type=jnp.float32)
    partial_a = inner_cols(weights[0], recv_rows).reshape(nz, ny, half, width)
    weight_b, rows_b, total = lax.optimization_barrier((weights[1], recv_rows, total))
    partial_b = inner_cols(weight_b, rows_b).reshape(ny, nz, half, width)
    grad_a, grad_b = reduce_pair(partial_a, partial_b, nz, ny)
    caption_grad = jnp.concatenate([grad_a, grad_b], axis=0)
    return (clip_grad, caption_grad)


def solution(mesh):
    placed = (
        P(("grp", "mem"), None),
        P(("grp", "mem"), None),
        P(("grp", "mem")),
        P(("grp", "mem")),
        P(("grp", "mem")),
        P(),
        P(),
        P(),
    )
    return jax.shard_map(
        inner_body,
        mesh=mesh,
        in_specs=placed,
        out_specs=(P(("grp", "mem"), None), P(("grp", "mem"), None)),
        check_vma=False,
    )
```

```python
import jax
import jax.numpy as jnp
from jax import lax
from jax.sharding import PartitionSpec as P


def pair_weights(logits, matched, same):
    sign = jnp.where(matched, 1.0, -1.0).astype(jnp.float32)
    return jnp.where(same, -sign * jax.nn.sigmoid(-sign * logits), 0.0).astype(jnp.bfloat16)


def inner_rows(left, right):
    return lax.dot_general(
        left, right, (((1,), (1,)), ((), ())), preferred_element_type=jnp.float32
    )


def inner_cols(left, right):
    return lax.dot_general(
        left, right, (((0,), (0,)), ((), ())), preferred_element_type=jnp.float32
    )


def shift_pairs(nz, ny, d, along_y):
    pairs = []
    for z in range(nz):
        for y in range(ny):
            if along_y:
                pairs.append((z * ny + y, z * ny + (y + d) % ny))
            else:
                pairs.append((z * ny + y, ((z + d) % nz) * ny + y))
    return pairs


def gather_first(xa, xb, nz, ny):
    parts_a = [xa]
    parts_b = [xb]
    for d in range(1, ny):
        parts_a.append(lax.ppermute(xa, "mem", shift_pairs(nz, ny, d, True)))
        parts_b.append(lax.ppermute(xb, "mem", shift_pairs(nz, ny, d, False)))
    return jnp.stack(parts_a), jnp.stack(parts_b)


def gather_second(inner_a, inner_b, nz, ny):
    parts_a = [inner_a]
    parts_b = [inner_b]
    for d in range(1, nz):
        parts_a.append(lax.ppermute(inner_a, "mem", shift_pairs(nz, ny, d, False)))
        parts_b.append(lax.ppermute(inner_b, "mem", shift_pairs(nz, ny, d, True)))
    return jnp.stack(parts_a), jnp.stack(parts_b)


def reduce_pair(blocks_a, blocks_b, nz, ny):
    low = jnp.bfloat16
    total_a = blocks_a[0]
    total_b = blocks_b[0]
    for d in range(1, nz):
        total_a = total_a + lax.ppermute(blocks_a[d].astype(low), "mem", shift_pairs(nz, ny, -d, False)).astype(jnp.float32)
        total_b = total_b + lax.ppermute(blocks_b[d].astype(low), "mem", shift_pairs(nz, ny, -d, True)).astype(jnp.float32)
    out_a = total_a[0]
    out_b = total_b[0]
    for d in range(1, ny):
        out_a = out_a + lax.ppermute(total_a[d].astype(low), "mem", shift_pairs(nz, ny, -d, True)).astype(jnp.float32)
        out_b = out_b + lax.ppermute(total_b[d].astype(low), "mem", shift_pairs(nz, ny, -d, False)).astype(jnp.float32)
    return out_a, out_b


def inner_body(clips, captions, clip_bucket, clip_positive, caption_bucket, bucket_owner, scale, bias):
    groups = lax.axis_size("grp")
    members = lax.axis_size("mem")
    ny = int(round(members ** 0.5))
    nz = members // ny
    clip_rows, width = clips.shape
    cap_rows = captions.shape[0]
    half = cap_rows // 2
    n_buckets = bucket_owner.shape[0]
    capacity = clip_rows // members * 4
    slots = capacity * groups
    panel = cap_rows * members
    mult = scale[0]
    shift = bias[0]
    group_index = lax.axis_index("grp")
    member = lax.axis_index("mem")
    my_z = member // ny
    my_y = member % ny
    tags = caption_bucket.astype(captions.dtype).reshape(2, half).T
    tag_a = jnp.concatenate([tags, jnp.zeros((half, 126), captions.dtype)], axis=1)
    own_a = jnp.concatenate([captions[:half], tag_a], axis=1)
    inner_a, inner_b = gather_first(own_a, captions[half:], nz, ny)
    got_a, got_b = gather_second(inner_a, inner_b, nz, ny)
    bucket_hot = clip_bucket[:, None] == jnp.arange(n_buckets, dtype=jnp.int32)[None, :]
    owner = jnp.sum(jnp.where(bucket_hot, bucket_owner[None, :], 0), axis=1)
    onehot = (owner[:, None] == jnp.arange(groups, dtype=jnp.int32)[None, :]).astype(jnp.int32)
    before = jnp.cumsum(onehot, axis=0) - onehot
    rank = jnp.sum(before * onehot, axis=1)
    position = owner * capacity + rank
    meta = jnp.stack(
        [clip_bucket + 1, clip_positive // 128, clip_positive % 128], axis=1
    ).astype(clips.dtype)
    extra = jnp.concatenate([jnp.zeros((clip_rows, 1), clips.dtype), meta,
                             jnp.zeros((clip_rows, 124), clips.dtype)], axis=1)
    placer = (position[:, None] == jnp.arange(slots, dtype=jnp.int32)[None, :]).astype(clips.dtype)
    send_rows = lax.dot_general(
        placer, jnp.concatenate([clips, extra], axis=1), (((0,), (0,)), ((), ())),
        preferred_element_type=jnp.float32,
    ).astype(clips.dtype)
    recv_ext = lax.all_to_all(send_rows, "grp", split_axis=0, concat_axis=0, tiled=True)
    recv_rows = recv_ext[:, :width]
    recv_meta = recv_ext[:, width + 1:width + 4].astype(jnp.int32)
    recv_bucket = recv_meta[:, 0] - 1
    recv_positive = jnp.where(recv_bucket >= 0, recv_meta[:, 1] * 128 + recv_meta[:, 2], -1)
    bucket_a = got_a[..., width].reshape(-1).astype(jnp.int32)
    bucket_b = jnp.swapaxes(got_a[..., width + 1], 0, 1).reshape(-1).astype(jnp.int32)
    got_a = got_a.reshape(members * half, -1)
    got_b = got_b.reshape(members * half, -1)
    ar = jnp.arange(half, dtype=jnp.int32)
    za = jnp.arange(nz, dtype=jnp.int32)
    ya = jnp.arange(ny, dtype=jnp.int32)
    src_a = ((my_z - za[:, None]) % nz) * ny + (my_y - ya[None, :]) % ny
    src_b = ((my_z - za[None, :]) % nz) * ny + (my_y - ya[:, None]) % ny
    base = group_index * panel
    ids_a = (base + src_a[:, :, None] * cap_rows + ar[None, None, :]).reshape(-1)
    ids_b = (base + src_b[:, :, None] * cap_rows + half + ar[None, None, :]).reshape(-1)
    weights = []
    rows = []
    for got, ids, bucket_y in ((got_a, ids_a, bucket_a), (got_b, ids_b, bucket_b)):
        rows_y = got[:, :width]
        logits = mult * inner_rows(recv_rows, rows_y) + shift
        weights.append(pair_weights(
            logits, recv_positive[:, None] == ids[None, :], recv_bucket[:, None] == bucket_y[None, :]
        ))
        rows.append(rows_y)
    total = (jnp.dot(weights[0], rows[0], preferred_element_type=jnp.float32)
             + jnp.dot(weights[1], rows[1], preferred_element_type=jnp.float32))
    returned = lax.all_to_all(total.astype(jnp.bfloat16), "grp", split_axis=0, concat_axis=0, tiled=True)
    clip_grad = jnp.dot(placer, returned, preferred_element_type=jnp.float32)
    partial_a = inner_cols(weights[0], recv_rows).reshape(nz, ny, half, width)
    weight_b, rows_b, total = lax.optimization_barrier((weights[1], recv_rows, total))
    partial_b = inner_cols(weight_b, rows_b).reshape(ny, nz, half, width)
    grad_a, grad_b = reduce_pair(partial_a, partial_b, nz, ny)
    caption_grad = jnp.concatenate([grad_a, grad_b], axis=0)
    return (clip_grad, caption_grad)


def solution(mesh):
    placed = (
        P(("grp", "mem"), None),
        P(("grp", "mem"), None),
        P(("grp", "mem")),
        P(("grp", "mem")),
        P(("grp", "mem")),
        P(),
        P(),
        P(),
    )
    return jax.shard_map(
        inner_body,
        mesh=mesh,
        in_specs=placed,
        out_specs=(P(("grp", "mem"), None), P(("grp", "mem"), None)),
        check_vma=False,
    )
```

```python
import jax
import jax.numpy as jnp
from jax import lax
from jax.sharding import PartitionSpec as P


def pair_weights(logits, matched, same):
    sign = jnp.where(matched, 1.0, -1.0).astype(jnp.float32)
    return jnp.where(same, -sign * jax.nn.sigmoid(-sign * logits), 0.0).astype(jnp.bfloat16)


def inner_rows(left, right):
    return lax.dot_general(
        left, right, (((1,), (1,)), ((), ())), preferred_element_type=jnp.float32
    )


def inner_cols(left, right):
    return lax.dot_general(
        left, right, (((0,), (0,)), ((), ())), preferred_element_type=jnp.float32
    )


def shift_pairs(nz, ny, d, along_y):
    pairs = []
    for z in range(nz):
        for y in range(ny):
            if along_y:
                pairs.append((z * ny + y, z * ny + (y + d) % ny))
            else:
                pairs.append((z * ny + y, ((z + d) % nz) * ny + y))
    return pairs


def gather_first(xa, xb, nz, ny):
    parts_a = [xa]
    parts_b = [xb]
    for d in range(1, ny):
        parts_a.append(lax.ppermute(xa, "mem", shift_pairs(nz, ny, d, True)))
        parts_b.append(lax.ppermute(xb, "mem", shift_pairs(nz, ny, d, False)))
    return jnp.stack(parts_a), jnp.stack(parts_b)


def gather_second(inner_a, inner_b, nz, ny):
    parts_a = [inner_a]
    parts_b = [inner_b]
    for d in range(1, nz):
        parts_a.append(lax.ppermute(inner_a, "mem", shift_pairs(nz, ny, d, False)))
        parts_b.append(lax.ppermute(inner_b, "mem", shift_pairs(nz, ny, d, True)))
    return jnp.stack(parts_a), jnp.stack(parts_b)


def reduce_pair(blocks_a, blocks_b, nz, ny):
    low = jnp.bfloat16
    total_a = blocks_a[0]
    total_b = blocks_b[0]
    for d in range(1, nz):
        total_a = total_a + lax.ppermute(blocks_a[d].astype(low), "mem", shift_pairs(nz, ny, -d, False)).astype(jnp.float32)
        total_b = total_b + lax.ppermute(blocks_b[d].astype(low), "mem", shift_pairs(nz, ny, -d, True)).astype(jnp.float32)
    out_a = total_a[0]
    out_b = total_b[0]
    for d in range(1, ny):
        out_a = out_a + lax.ppermute(total_a[d].astype(low), "mem", shift_pairs(nz, ny, -d, True)).astype(jnp.float32)
        out_b = out_b + lax.ppermute(total_b[d].astype(low), "mem", shift_pairs(nz, ny, -d, False)).astype(jnp.float32)
    return out_a, out_b


def inner_body(clips, captions, clip_bucket, clip_positive, caption_bucket, bucket_owner, scale, bias):
    groups = lax.axis_size("grp")
    members = lax.axis_size("mem")
    ny = int(round(members ** 0.5))
    nz = members // ny
    clip_rows, width = clips.shape
    cap_rows = captions.shape[0]
    half = cap_rows // 2
    n_buckets = bucket_owner.shape[0]
    capacity = clip_rows // members * 4
    slots = capacity * groups
    panel = cap_rows * members
    mult = scale[0]
    shift = bias[0]
    group_index = lax.axis_index("grp")
    member = lax.axis_index("mem")
    my_z = member // ny
    my_y = member % ny
    tags = caption_bucket.astype(captions.dtype).reshape(2, half).T
    tag_a = jnp.concatenate([tags, jnp.zeros((half, 126), captions.dtype)], axis=1)
    own_a = jnp.concatenate([captions[:half], tag_a], axis=1)
    inner_a, inner_b = gather_first(own_a, captions[half:], nz, ny)
    got_a, got_b = gather_second(inner_a, inner_b, nz, ny)
    bucket_hot = clip_bucket[:, None] == jnp.arange(n_buckets, dtype=jnp.int32)[None, :]
    owner = jnp.sum(jnp.where(bucket_hot, bucket_owner[None, :], 0), axis=1)
    onehot = (owner[:, None] == jnp.arange(groups, dtype=jnp.int32)[None, :]).astype(clips.dtype)
    local = jnp.arange(clip_rows, dtype=jnp.int32)
    earlier = (local[:, None] > local[None, :]).astype(clips.dtype)
    before = jnp.dot(earlier, onehot, preferred_element_type=jnp.float32)
    rank = jnp.sum(before * onehot.astype(jnp.float32), axis=1).astype(jnp.int32)
    position = owner * capacity + rank
    meta = jnp.stack(
        [clip_bucket + 1, clip_positive // 128, clip_positive % 128], axis=1
    ).astype(clips.dtype)
    extra = jnp.concatenate([jnp.zeros((clip_rows, 1), clips.dtype), meta,
                             jnp.zeros((clip_rows, 124), clips.dtype)], axis=1)
    placer = (position[:, None] == jnp.arange(slots, dtype=jnp.int32)[None, :]).astype(clips.dtype)
    send_rows = lax.dot_general(
        placer, jnp.pad(clips, ((0, 0), (0, 128))) + jnp.pad(extra, ((0, 0), (width, 0))), (((0,), (0,)), ((), ())),
        preferred_element_type=jnp.float32,
    ).astype(clips.dtype)
    recv_ext = lax.all_to_all(send_rows, "grp", split_axis=0, concat_axis=0, tiled=True)
    recv_rows = recv_ext[:, :width]
    recv_meta = recv_ext[:, width + 1:width + 4].astype(jnp.int32)
    recv_bucket = recv_meta[:, 0] - 1
    recv_positive = jnp.where(recv_bucket >= 0, recv_meta[:, 1] * 128 + recv_meta[:, 2], -1)
    bucket_a = got_a[..., width].reshape(-1).astype(jnp.int32)
    bucket_b = jnp.swapaxes(got_a[..., width + 1], 0, 1).reshape(-1).astype(jnp.int32)
    got_a = got_a.reshape(members * half, -1)
    got_b = got_b.reshape(members * half, -1)
    ar = jnp.arange(half, dtype=jnp.int32)
    za = jnp.arange(nz, dtype=jnp.int32)
    ya = jnp.arange(ny, dtype=jnp.int32)
    src_a = ((my_z - za[:, None]) % nz) * ny + (my_y - ya[None, :]) % ny
    src_b = ((my_z - za[None, :]) % nz) * ny + (my_y - ya[:, None]) % ny
    base = group_index * panel
    ids_a = (base + src_a[:, :, None] * cap_rows + ar[None, None, :]).reshape(-1)
    ids_b = (base + src_b[:, :, None] * cap_rows + half + ar[None, None, :]).reshape(-1)
    weights = []
    rows = []
    for got, ids, bucket_y in ((got_a, ids_a, bucket_a), (got_b, ids_b, bucket_b)):
        rows_y = got[:, :width]
        logits = mult * inner_rows(recv_rows, rows_y) + shift
        weights.append(pair_weights(
            logits, recv_positive[:, None] == ids[None, :], recv_bucket[:, None] == bucket_y[None, :]
        ))
        rows.append(rows_y)
    total = (jnp.dot(weights[0], rows[0], preferred_element_type=jnp.float32)
             + jnp.dot(weights[1], rows[1], preferred_element_type=jnp.float32))
    returned = lax.all_to_all(total.astype(jnp.bfloat16), "grp", split_axis=0, concat_axis=0, tiled=True)
    clip_grad = jnp.dot(placer, returned, preferred_element_type=jnp.float32)
    partial_a = inner_cols(weights[0], recv_rows).reshape(nz, ny, half, width)
    weight_b, rows_b, total = lax.optimization_barrier((weights[1], recv_rows, total))
    partial_b = inner_cols(weight_b, rows_b).reshape(ny, nz, half, width)
    grad_a, grad_b = reduce_pair(partial_a, partial_b, nz, ny)
    caption_grad = jnp.concatenate([grad_a, grad_b], axis=0)
    return (clip_grad, caption_grad)


def solution(mesh):
    placed = (
        P(("grp", "mem"), None),
        P(("grp", "mem"), None),
        P(("grp", "mem")),
        P(("grp", "mem")),
        P(("grp", "mem")),
        P(),
        P(),
        P(),
    )
    return jax.shard_map(
        inner_body,
        mesh=mesh,
        in_specs=placed,
        out_specs=(P(("grp", "mem"), None), P(("grp", "mem"), None)),
        check_vma=False,
    )
```
